32 devices in a mesh: uv: 8 (over z, y), rep: 4 (over x, core).
Axes of the slice: x: 2, y: 2, z: 4, core: 2. Of those that a mesh axis runs over, the one named last changes fastest.
Arguments:
- visibilities: float32 [2, 32, 8, 16, 12], P(None, ('uv', 'rep')), may hold values from -6 to 6
- tile_counts: int32 [32, 8, 16], P(('uv', 'rep')), may hold values from 2 to 12, as said below
- w_plane: int32 [32, 8, 16, 12], P(('uv', 'rep')), may hold values from 0 to 63
- u_offset: int32 [32, 8, 16, 12], P(('uv', 'rep')), may hold values from 0 to 120
- v_offset: int32 [32, 8, 16, 12], P(('uv', 'rep')), may hold values from 0 to 120
- kernels: float32 [64, 128], replicated, may hold values from -2.5 to 2.5
Outputs:
- spectrum: float32 [2048, 2, 1024], P(('uv', 'rep'))
The draws below stay inside these ranges and needn't reach their ends.
Inputs may be any that keep to these rules, and one draw needn't show every extreme that they name: `tile_counts`: every source device's list for tile 16//2 of destination column 4 holds 12 visibilities; tiles near the grid's centre are fuller than others.
All inputs are finite; a program needn't handle non-finite values.
Results may differ from the reference program's by a relative error of at most 0.0029.
Values may be sent and summed in bfloat16 or wider, within the bound.
No kernel may reach another device: no remote copies, remote signals or barrier semaphores. Data moves between devices by JAX's collectives and lax.ppermute only.
A program may use at most 192 MiB of HBM per device.

```python
import math
import jax
import jax.numpy as jnp
from jax import lax

TILE = 128
SUPPORT = 8
WPLANES = 64
TU = 16
SLOT_CAPACITY = 12
DESTS = 8
SOURCES = 32


def draw_tile_counts(key, part):
    first_key, second_random_key = jax.random.split(key)
    array_shape = (SOURCES, DESTS, TU)
    base_amount = jax.random.randint(first_key, array_shape, 2, SLOT_CAPACITY // 2 + 1)
    extra_amount = jax.random.randint(second_random_key, array_shape, 0, SLOT_CAPACITY - SLOT_CAPACITY // 2 + 1)
    dest_index = lax.broadcasted_iota(jnp.int32, array_shape, 1)
    tile_index = lax.broadcasted_iota(jnp.int32, array_shape, 2)
    central_value = (dest_index >= DESTS // 4) & (dest_index < DESTS - DESTS // 4) & (tile_index >= TU // 4) & (tile_index < TU - TU // 4)
    slot_counts = jnp.minimum(base_amount + jnp.where(central_value, extra_amount, 0), SLOT_CAPACITY)
    hottest = (dest_index == DESTS // 2) & (tile_index == TU // 2)
    return jnp.where(hottest, SLOT_CAPACITY, slot_counts).astype(jnp.int32)


def with_ends(result, own_key, least, top_value):
    index_at = [jax.random.randint(jax.random.fold_in(own_key, axis), (), 0, length) for axis, length in enumerate(result.shape)]
    widest = result.shape.index(max(result.shape))
    neighbour = index_at[:widest] + [(index_at[widest] + 1) % result.shape[widest]] + index_at[widest + 1:]
    return result.at[tuple(index_at)].set(least).at[tuple(neighbour)].set(top_value)


def levels(own_key, dims, pieces, low, largest):
    level, own = 1.0, jax.random.fold_in(own_key, 6)
    for position, shards_of in pieces:
        steps = jnp.exp(jax.random.uniform(jax.random.fold_in(own, position), (shards_of,), jnp.float32, low / len(pieces), largest / len(pieces)))
        level = level * jnp.repeat(steps, dims[position] // shards_of).reshape([-1 if axis == position else 1 for axis in range(len(dims))])
    return level


def normal_values(own_key, shape, deviation, bound, cuts=(), kind=jnp.bfloat16):
    array = jax.random.normal(own_key, shape, jnp.float32) * deviation
    if len(cuts) > 0:
        array = levels(own_key, shape, cuts, -0.22, 0.18) * array
    return jnp.clip(array, min=-bound, max=bound).astype(kind)


def setup_inputs(seed: int = 0) -> dict:
    key_of = jax.random.split(jax.random.key(seed), 7)
    return {
        "visibilities": normal_values(key_of[0], (2, SOURCES, DESTS, TU, SLOT_CAPACITY), 1.0, 6.0, ((1, 32),), jnp.float32),
        "tile_counts": draw_tile_counts(jax.random.fold_in(key_of[6], 71), 0),
        "w_plane": with_ends(jax.random.randint(key_of[2], (SOURCES, DESTS, TU, SLOT_CAPACITY), 0, WPLANES), jax.random.fold_in(key_of[2], 1), 0, WPLANES - 1).astype(jnp.int32),
        "u_offset": with_ends(jax.random.randint(key_of[3], (SOURCES, DESTS, TU, SLOT_CAPACITY), 0, TILE - SUPPORT + 1), jax.random.fold_in(key_of[3], 1), 0, TILE - SUPPORT).astype(jnp.int32),
        "v_offset": with_ends(jax.random.randint(key_of[4], (SOURCES, DESTS, TU, SLOT_CAPACITY), 0, TILE - SUPPORT + 1), jax.random.fold_in(key_of[4], 1), 0, TILE - SUPPORT).astype(jnp.int32),
        "kernels": normal_values(key_of[5], (WPLANES, 2 * SUPPORT * SUPPORT), 0.35, 2.5, (), jnp.float32),
    }


def reference(visibilities, tile_counts, w_plane, u_offset, v_offset, kernels):
    array_shape = (DESTS, TU, SLOT_CAPACITY)
    slots = lax.broadcasted_iota(jnp.int32, array_shape, 2)
    dest_index = lax.broadcasted_iota(jnp.int32, array_shape, 0)
    tile_index = lax.broadcasted_iota(jnp.int32, array_shape, 1)
    taps = jnp.arange(SUPPORT, dtype=jnp.int32)
    half = SUPPORT * SUPPORT
    table = kernels
    full = array_shape + (SUPPORT, SUPPORT)

    def add_source(source, grids):
        grid_re, grid_im = grids
        live = (slots < tile_counts[source][:, :, None]).astype(table.dtype)
        vis_re = visibilities[0, source] * live
        vis_im = visibilities[1, source] * live
        kern = table[w_plane[source]]
        kern_re = kern[..., :half]
        kern_im = kern[..., half:]
        part_re = (vis_re[..., None] * kern_re - vis_im[..., None] * kern_im).astype(jnp.bfloat16)
        part_im = (vis_re[..., None] * kern_im + vis_im[..., None] * kern_re).astype(jnp.bfloat16)
        part_re, part_im = lax.optimization_barrier((part_re, part_im))
        part_re = part_re.astype(grid_re.dtype).reshape(full)
        part_im = part_im.astype(grid_re.dtype).reshape(full)
        row_ids = (tile_index * TILE + u_offset[source])[..., None, None] + taps[:, None]
        col_ids = (dest_index * TILE + v_offset[source])[..., None, None] + taps[None, :]
        row_ids = jnp.broadcast_to(row_ids, full)
        col_ids = jnp.broadcast_to(col_ids, full)
        grid_re = grid_re.at[row_ids, col_ids].add(part_re)
        grid_im = grid_im.at[row_ids, col_ids].add(part_im)
        return (grid_re, grid_im)
    zeros = jnp.zeros((TU * TILE, DESTS * TILE), dtype=kernels.dtype)
    grid_re, grid_im = lax.fori_loop(0, SOURCES, add_source, (zeros, zeros))
    spectrum = jnp.fft.fft(grid_re + 1j * grid_im, axis=1) / math.sqrt(DESTS * TILE)
    return jnp.stack([jnp.real(spectrum), jnp.imag(spectrum)], axis=1).astype(jnp.float32)
```

```python
import functools
import math

import jax
import jax.numpy as jnp
from jax import lax
from jax.experimental import pallas as pl
from jax.experimental.pallas import tpu as pltpu
from jax.sharding import PartitionSpec as P

TILE = 128
SUPPORT = 8
GROUP = 16
FIELDS = 5


def make_table(first, second, length):
    index_a = lax.broadcasted_iota(jnp.int32, (first, second), 0)
    index_b = lax.broadcasted_iota(jnp.int32, (first, second), 1)
    angle = 2.0 * math.pi / length * (index_a * index_b % length).astype(jnp.float32)
    return (jnp.cos(angle), jnp.sin(angle))


def transform(real_in, imag_in, groups):
    nrows = real_in.shape[0]
    total = real_in.shape[1]
    width = total // groups
    highest = lax.Precision.HIGHEST
    cos_a, sin_a = make_table(groups, groups, groups)
    cos_t, sin_t = make_table(groups, width, total)
    cos_b, sin_b = make_table(width, width, width)
    real_in = real_in.reshape(nrows, groups, width)
    imag_in = imag_in.reshape(nrows, groups, width)
    first_re = jnp.einsum("rpj,pk->rkj", real_in, cos_a, precision=highest) + jnp.einsum(
        "rpj,pk->rkj", imag_in, sin_a, precision=highest
    )
    first_im = jnp.einsum("rpj,pk->rkj", imag_in, cos_a, precision=highest) - jnp.einsum(
        "rpj,pk->rkj", real_in, sin_a, precision=highest
    )
    turned_re = first_re * cos_t + first_im * sin_t
    turned_im = first_im * cos_t - first_re * sin_t
    final_re = jnp.einsum("rkj,jm->rmk", turned_re, cos_b, precision=highest) + jnp.einsum(
        "rkj,jm->rmk", turned_im, sin_b, precision=highest
    )
    final_im = jnp.einsum("rkj,jm->rmk", turned_im, cos_b, precision=highest) - jnp.einsum(
        "rkj,jm->rmk", turned_re, sin_b, precision=highest
    )
    scale = 1.0 / math.sqrt(total)
    return (
        jnp.stack([final_re.reshape(nrows, total), final_im.reshape(nrows, total)], axis=1) * scale
    )


def weigh(vis_re, vis_im, planes, kernels):
    nplanes = kernels.shape[0]
    width = kernels.shape[1]
    half = width // 2
    onehot = (
        planes[..., None] == lax.broadcasted_iota(jnp.int32, planes.shape + (nplanes,), planes.ndim)
    ).astype(jnp.float32)
    kern = jnp.dot(
        onehot.reshape(-1, nplanes),
        kernels,
        precision=lax.Precision.HIGHEST,
        preferred_element_type=jnp.float32,
    )
    kern = kern.reshape(planes.shape + (width,))
    kern_re = kern[..., :half]
    kern_im = kern[..., half:]
    part_re = vis_re[..., None] * kern_re - vis_im[..., None] * kern_im
    part_im = vis_re[..., None] * kern_im + vis_im[..., None] * kern_re
    return jnp.concatenate([part_re, part_im], axis=-1).astype(jnp.bfloat16)


def grid_kernel(w_ref, vob_ref, uoa_ref, e_ref, out_ref, rep_ref):
    chunk_step = pl.program_id(1)
    chunk = w_ref.shape[1]
    rows = out_ref.shape[1]
    ngroups = chunk // GROUP
    nblocks = w_ref.shape[2] // SUPPORT

    @pl.when(chunk_step == 0)
    def _():
        out_ref[...] = jnp.zeros_like(out_ref)

    rep_ref[...] = jnp.dot(
        w_ref[0], e_ref[...], preferred_element_type=jnp.float32
    ).astype(jnp.bfloat16)
    lane = lax.broadcasted_iota(jnp.int32, (GROUP, TILE), 1)
    row = lax.broadcasted_iota(jnp.int32, (GROUP, TILE), 0)
    keep = (lane // SUPPORT) == row
    vrow = lax.broadcasted_iota(jnp.int32, (TILE, TILE), 0)
    urow = lax.broadcasted_iota(jnp.int32, (rows, TILE), 0)
    zero = jnp.zeros((GROUP, TILE), jnp.bfloat16)

    def body(g, acc):
        start = pl.multiple_of(g * GROUP, GROUP)
        blocks = [
            jnp.where(keep, rep_ref[pl.ds(start, GROUP), pl.ds(i * TILE, TILE)], zero)
            for i in range(nblocks)
        ]
        wbd = jnp.concatenate(blocks, axis=0)
        vob = vob_ref[0, pl.ds(g, 1), :]
        cst = (vrow == vob).astype(jnp.bfloat16)
        spread = lax.dot_general(
            wbd, cst, (((1,), (1,)), ((), ())), preferred_element_type=jnp.float32
        ).astype(jnp.bfloat16)
        uoa = uoa_ref[0, pl.ds(g, 1), :]
        pick = (urow == uoa).astype(jnp.bfloat16)
        half = spread.shape[0] // 2
        acc_re = acc[0] + jnp.dot(pick, spread[:half], preferred_element_type=jnp.float32)
        acc_im = acc[1] + jnp.dot(pick, spread[half:], preferred_element_type=jnp.float32)
        return (acc_re, acc_im)

    init = (jnp.zeros((rows, TILE), jnp.float32), jnp.zeros((rows, TILE), jnp.float32))
    acc_re, acc_im = lax.fori_loop(0, ngroups, body, init)
    out_ref[0] += acc_re
    out_ref[1] += acc_im


def grid_rows(weighted, vob, uoa, rows):
    dests, per_dest, width = weighted.shape
    chunk = per_dest
    for size in (384, 192, 96, 48, 16):
        if per_dest % size == 0 and size <= per_dest:
            chunk = size
            break
    steps = per_dest // chunk
    nblocks = width // SUPPORT
    lanes_in = lax.broadcasted_iota(jnp.int32, (width, nblocks * TILE), 0)
    lanes_out = lax.broadcasted_iota(jnp.int32, (width, nblocks * TILE), 1)
    expand = (
        (lanes_in // SUPPORT == lanes_out // TILE) & (lanes_in % SUPPORT == lanes_out % SUPPORT)
    ).astype(jnp.bfloat16)
    return pl.pallas_call(
        grid_kernel,
        grid=(dests, steps),
        in_specs=[
            pl.BlockSpec((1, chunk, width), lambda d, c: (d, c, 0)),
            pl.BlockSpec((1, chunk // GROUP, TILE), lambda d, c: (d, c, 0)),
            pl.BlockSpec((1, chunk // GROUP, TILE), lambda d, c: (d, c, 0)),
            pl.BlockSpec((width, nblocks * TILE), lambda d, c: (0, 0)),
        ],
        out_specs=pl.BlockSpec((2, rows, TILE), lambda d, c: (0, 0, d)),
        out_shape=jax.ShapeDtypeStruct((2, rows, dests * TILE), jnp.float32),
        scratch_shapes=[pltpu.VMEM((chunk, nblocks * TILE), jnp.bfloat16)],
        compiler_params=pltpu.CompilerParams(
            dimension_semantics=("arbitrary", "arbitrary")
        ),
    )(weighted, vob, uoa, expand)


def shards(visibilities, tile_counts, w_plane, u_offset, v_offset, kernels):
    dests = visibilities.shape[2]
    ntiles = visibilities.shape[3]
    slots = visibilities.shape[4]
    axes = ("uv", "rep")
    ndev = lax.axis_size(axes)
    rows = ntiles * TILE // ndev
    per_tile = ndev // ntiles
    me = lax.axis_index(axes)
    live = (
        lax.broadcasted_iota(jnp.int32, (dests, ntiles, slots), 2) < tile_counts[0][:, :, None]
    ).astype(jnp.float32)
    fields = jnp.stack(
        [
            visibilities[0, 0] * live,
            visibilities[1, 0] * live,
            w_plane[0].astype(jnp.float32),
            u_offset[0].astype(jnp.float32),
            v_offset[0].astype(jnp.float32),
        ]
    )
    send = jnp.repeat(fields, per_tile, axis=2)
    send = jnp.moveaxis(send, 2, 0)
    got = lax.all_to_all(send, axes, split_axis=0, concat_axis=0, tiled=True)
    got = jnp.moveaxis(got, 0, 2).reshape(FIELDS, dests, ndev * slots)
    vis_re = got[0]
    vis_im = got[1]
    planes = got[2].astype(jnp.int32)
    rows_first = got[3].astype(jnp.int32)
    cols_first = got[4].astype(jnp.int32)
    if vis_re.size <= 65536:
        weighted = weigh(vis_re, vis_im, planes, kernels)
    else:
        weighted = lax.map(lambda x: weigh(x[0], x[1], x[2], kernels), (vis_re, vis_im, planes))
    per_dest = ndev * slots
    ngroups = per_dest // GROUP
    taps = jnp.arange(SUPPORT, dtype=jnp.int32)
    vob = (cols_first.reshape(dests, ngroups, GROUP, 1) + taps).reshape(dests, ngroups, TILE)
    offset = (me % per_tile) * rows
    uoa = (rows_first.reshape(dests, ngroups, 1, GROUP) + taps[:, None] - offset).reshape(
        dests, ngroups, TILE
    )
    slab = grid_rows(weighted, vob, uoa, rows)
    return transform(slab[0], slab[1], dests)


def solution(mesh):
    placed = (
        P(None, ("uv", "rep"), None, None, None),
        P(("uv", "rep"), None, None),
        P(("uv", "rep"), None, None, None),
        P(("uv", "rep"), None, None, None),
        P(("uv", "rep"), None, None, None),
        P(),
    )
    return jax.shard_map(
        shards, mesh=mesh, in_specs=placed, out_specs=P(("uv", "rep"), None, None), check_vma=False
    )
```

```python
import functools
import math

import jax
import jax.numpy as jnp
from jax import lax
from jax.experimental import pallas as pl
from jax.experimental.pallas import tpu as pltpu
from jax.sharding import PartitionSpec as P

TILE = 128
SUPPORT = 8
GROUP = 16
FIELDS = 5


def make_table(first, second, length):
    index_a = lax.broadcasted_iota(jnp.int32, (first, second), 0)
    index_b = lax.broadcasted_iota(jnp.int32, (first, second), 1)
    angle = 2.0 * math.pi / length * (index_a * index_b % length).astype(jnp.float32)
    return (jnp.cos(angle), jnp.sin(angle))


def transform(real_in, imag_in, groups):
    nrows = real_in.shape[0]
    total = real_in.shape[1]
    width = total // groups
    highest = lax.Precision.HIGHEST
    cos_a, sin_a = make_table(groups, groups, groups)
    cos_t, sin_t = make_table(groups, width, total)
    cos_b, sin_b = make_table(width, width, width)
    real_in = real_in.reshape(nrows, groups, width)
    imag_in = imag_in.reshape(nrows, groups, width)
    first_re = jnp.einsum("rpj,pk->rkj", real_in, cos_a, precision=highest) + jnp.einsum(
        "rpj,pk->rkj", imag_in, sin_a, precision=highest
    )
    first_im = jnp.einsum("rpj,pk->rkj", imag_in, cos_a, precision=highest) - jnp.einsum(
        "rpj,pk->rkj", real_in, sin_a, precision=highest
    )
    turned_re = first_re * cos_t + first_im * sin_t
    turned_im = first_im * cos_t - first_re * sin_t
    final_re = jnp.einsum("rkj,jm->rmk", turned_re, cos_b, precision=highest) + jnp.einsum(
        "rkj,jm->rmk", turned_im, sin_b, precision=highest
    )
    final_im = jnp.einsum("rkj,jm->rmk", turned_im, cos_b, precision=highest) - jnp.einsum(
        "rkj,jm->rmk", turned_re, sin_b, precision=highest
    )
    scale = 1.0 / math.sqrt(total)
    return (
        jnp.stack([final_re.reshape(nrows, total), final_im.reshape(nrows, total)], axis=1) * scale
    )


def weigh(vis_re, vis_im, planes, kernels):
    nplanes = kernels.shape[0]
    width = kernels.shape[1]
    half = width // 2
    onehot = (
        planes[..., None] == lax.broadcasted_iota(jnp.int32, planes.shape + (nplanes,), planes.ndim)
    ).astype(jnp.float32)
    kern = jnp.dot(
        onehot.reshape(-1, nplanes),
        kernels,
        precision=lax.Precision.HIGHEST,
        preferred_element_type=jnp.float32,
    )
    kern = kern.reshape(planes.shape + (width,))
    kern_re = kern[..., :half]
    kern_im = kern[..., half:]
    part_re = vis_re[..., None] * kern_re - vis_im[..., None] * kern_im
    part_im = vis_re[..., None] * kern_im + vis_im[..., None] * kern_re
    return jnp.concatenate([part_re, part_im], axis=-1).astype(jnp.bfloat16)


def grid_kernel(w_ref, vob_ref, uoa_ref, e_ref, out_ref, rep_ref, x_ref, r_ref):
    chunk_step = pl.program_id(1)
    chunk = w_ref.shape[1]
    rows = out_ref.shape[1]
    ngroups = chunk // GROUP
    nblocks = w_ref.shape[2] // SUPPORT
    depth = nblocks * GROUP // 2

    @pl.when(chunk_step == 0)
    def _():
        out_ref[...] = jnp.zeros_like(out_ref)

    rep_ref[...] = jnp.dot(
        w_ref[0], e_ref[...], preferred_element_type=jnp.float32
    ).astype(jnp.bfloat16)
    lane = lax.broadcasted_iota(jnp.int32, (GROUP, TILE), 1)
    row = lax.broadcasted_iota(jnp.int32, (GROUP, TILE), 0)
    keep = (lane // SUPPORT) == row
    vrow = lax.broadcasted_iota(jnp.int32, (TILE, TILE), 0)
    urow = lax.broadcasted_iota(jnp.int32, (rows, TILE), 0)
    zero = jnp.zeros((GROUP, TILE), jnp.bfloat16)

    def body(g, carry):
        start = pl.multiple_of(g * GROUP, GROUP)
        blocks = [
            jnp.where(keep, rep_ref[pl.ds(start, GROUP), pl.ds(i * TILE, TILE)], zero)
            for i in range(nblocks)
        ]
        wbd = jnp.concatenate(blocks, axis=0)
        vob = vob_ref[0, pl.ds(g, 1), :]
        cst = (vrow == vob).astype(jnp.bfloat16)
        spread = lax.dot_general(
            wbd, cst, (((1,), (1,)), ((), ())), preferred_element_type=jnp.float32
        ).astype(jnp.bfloat16)
        at = pl.multiple_of(g * depth, depth)
        x_ref[0, pl.ds(at, depth), :] = spread[:depth]
        x_ref[1, pl.ds(at, depth), :] = spread[depth:]
        uoa = uoa_ref[0, pl.ds(g, 1), :]
        r_ref[:, pl.ds(at, TILE)] = (urow == uoa).astype(jnp.bfloat16)
        return carry

    lax.fori_loop(0, ngroups, body, 0, unroll=4)
    pick = r_ref[...]
    out_ref[0] += jnp.dot(pick, x_ref[0], preferred_element_type=jnp.float32)
    out_ref[1] += jnp.dot(pick, x_ref[1], preferred_element_type=jnp.float32)


def grid_rows(weighted, vob, uoa, rows):
    dests, per_dest, width = weighted.shape
    chunk = per_dest
    for size in (384, 192, 96, 48, 16):
        if per_dest % size == 0 and size <= per_dest:
            chunk = size
            break
    steps = per_dest // chunk
    nblocks = width // SUPPORT
    lanes_in = lax.broadcasted_iota(jnp.int32, (width, nblocks * TILE), 0)
    lanes_out = lax.broadcasted_iota(jnp.int32, (width, nblocks * TILE), 1)
    expand = (
        (lanes_in // SUPPORT == lanes_out // TILE) & (lanes_in % SUPPORT == lanes_out % SUPPORT)
    ).astype(jnp.bfloat16)
    return pl.pallas_call(
        grid_kernel,
        grid=(dests, steps),
        in_specs=[
            pl.BlockSpec((1, chunk, width), lambda d, c: (d, c, 0)),
            pl.BlockSpec((1, chunk // GROUP, TILE), lambda d, c: (d, c, 0)),
            pl.BlockSpec((1, chunk // GROUP, TILE), lambda d, c: (d, c, 0)),
            pl.BlockSpec((width, nblocks * TILE), lambda d, c: (0, 0)),
        ],
        out_specs=pl.BlockSpec((2, rows, TILE), lambda d, c: (0, 0, d)),
        out_shape=jax.ShapeDtypeStruct((2, rows, dests * TILE), jnp.float32),
        scratch_shapes=[
            pltpu.VMEM((chunk, nblocks * TILE), jnp.bfloat16),
            pltpu.VMEM((2, chunk * SUPPORT, TILE), jnp.bfloat16),
            pltpu.VMEM((rows, chunk * SUPPORT), jnp.bfloat16),
        ],
        compiler_params=pltpu.CompilerParams(
            dimension_semantics=("arbitrary", "arbitrary")
        ),
    )(weighted, vob, uoa, expand)


def shards(visibilities, tile_counts, w_plane, u_offset, v_offset, kernels):
    dests = visibilities.shape[2]
    ntiles = visibilities.shape[3]
    slots = visibilities.shape[4]
    axes = ("uv", "rep")
    ndev = lax.axis_size(axes)
    rows = ntiles * TILE // ndev
    per_tile = ndev // ntiles
    me = lax.axis_index(axes)
    live = (
        lax.broadcasted_iota(jnp.int32, (dests, ntiles, slots), 2) < tile_counts[0][:, :, None]
    ).astype(jnp.float32)
    fields = jnp.stack(
        [
            visibilities[0, 0] * live,
            visibilities[1, 0] * live,
            w_plane[0].astype(jnp.float32),
            u_offset[0].astype(jnp.float32),
            v_offset[0].astype(jnp.float32),
        ]
    )
    send = jnp.repeat(fields, per_tile, axis=2)
    send = jnp.moveaxis(send, 2, 0)
    got = lax.all_to_all(send, axes, split_axis=0, concat_axis=0, tiled=True)
    got = jnp.moveaxis(got, 0, 2).reshape(FIELDS, dests, ndev * slots)
    vis_re = got[0]
    vis_im = got[1]
    planes = got[2].astype(jnp.int32)
    rows_first = got[3].astype(jnp.int32)
    cols_first = got[4].astype(jnp.int32)
    if vis_re.size <= 65536:
        weighted = weigh(vis_re, vis_im, planes, kernels)
    else:
        weighted = lax.map(lambda x: weigh(x[0], x[1], x[2], kernels), (vis_re, vis_im, planes))
    per_dest = ndev * slots
    ngroups = per_dest // GROUP
    taps = jnp.arange(SUPPORT, dtype=jnp.int32)
    vob = (cols_first.reshape(dests, ngroups, GROUP, 1) + taps).reshape(dests, ngroups, TILE)
    offset = (me % per_tile) * rows
    uoa = (rows_first.reshape(dests, ngroups, 1, GROUP) + taps[:, None] - offset).reshape(
        dests, ngroups, TILE
    )
    slab = grid_rows(weighted, vob, uoa, rows)
    return transform(slab[0], slab[1], dests)


def solution(mesh):
    placed = (
        P(None, ("uv", "rep"), None, None, None),
        P(("uv", "rep"), None, None),
        P(("uv", "rep"), None, None, None),
        P(("uv", "rep"), None, None, None),
        P(("uv", "rep"), None, None, None),
        P(),
    )
    return jax.shard_map(
        shards, mesh=mesh, in_specs=placed, out_specs=P(("uv", "rep"), None, None), check_vma=False
    )
```

```python
import functools
import math

import jax
import jax.numpy as jnp
from jax import lax
from jax.experimental import pallas as pl
from jax.experimental.pallas import tpu as pltpu
from jax.sharding import PartitionSpec as P

TILE = 128
SUPPORT = 8
GROUP = 16
FIELDS = 5


def make_table(first, second, length):
    index_a = lax.broadcasted_iota(jnp.int32, (first, second), 0)
    index_b = lax.broadcasted_iota(jnp.int32, (first, second), 1)
    angle = 2.0 * math.pi / length * (index_a * index_b % length).astype(jnp.float32)
    return (jnp.cos(angle), jnp.sin(angle))


def transform(real_in, imag_in, groups):
    nrows = real_in.shape[0]
    total = real_in.shape[1]
    width = total // groups
    highest = lax.Precision.HIGHEST
    cos_a, sin_a = make_table(groups, groups, groups)
    cos_t, sin_t = make_table(groups, width, total)
    cos_b, sin_b = make_table(width, width, width)
    real_in = real_in.reshape(nrows, groups, width)
    imag_in = imag_in.reshape(nrows, groups, width)
    first_re = jnp.einsum("rpj,pk->rkj", real_in, cos_a, precision=highest) + jnp.einsum(
        "rpj,pk->rkj", imag_in, sin_a, precision=highest
    )
    first_im = jnp.einsum("rpj,pk->rkj", imag_in, cos_a, precision=highest) - jnp.einsum(
        "rpj,pk->rkj", real_in, sin_a, precision=highest
    )
    turned_re = first_re * cos_t + first_im * sin_t
    turned_im = first_im * cos_t - first_re * sin_t
    final_re = jnp.einsum("rkj,jm->rmk", turned_re, cos_b, precision=highest) + jnp.einsum(
        "rkj,jm->rmk", turned_im, sin_b, precision=highest
    )
    final_im = jnp.einsum("rkj,jm->rmk", turned_im, cos_b, precision=highest) - jnp.einsum(
        "rkj,jm->rmk", turned_re, sin_b, precision=highest
    )
    scale = 1.0 / math.sqrt(total)
    return (
        jnp.stack([final_re.reshape(nrows, total), final_im.reshape(nrows, total)], axis=1) * scale
    )


def weigh(vis_re, vis_im, planes, kernels):
    nplanes = kernels.shape[0]
    width = kernels.shape[1]
    half = width // 2
    onehot = (
        planes[..., None] == lax.broadcasted_iota(jnp.int32, planes.shape + (nplanes,), planes.ndim)
    ).astype(jnp.float32)
    kern = jnp.dot(
        onehot.reshape(-1, nplanes),
        kernels,
        precision=lax.Precision.HIGHEST,
        preferred_element_type=jnp.float32,
    )
    kern = kern.reshape(planes.shape + (width,))
    kern_re = kern[..., :half]
    kern_im = kern[..., half:]
    part_re = vis_re[..., None] * kern_re - vis_im[..., None] * kern_im
    part_im = vis_re[..., None] * kern_im + vis_im[..., None] * kern_re
    return jnp.concatenate([part_re, part_im], axis=-1).astype(jnp.bfloat16)


def grid_kernel(w_ref, vob_ref, uoa_ref, e_ref, out_ref, rep_ref, x_ref, r_ref):
    chunk_step = pl.program_id(1)
    chunk = w_ref.shape[1]
    rows = out_ref.shape[1]
    ngroups = chunk // GROUP
    nblocks = w_ref.shape[2] // SUPPORT
    depth = nblocks * GROUP // 2

    @pl.when(chunk_step == 0)
    def _():
        out_ref[...] = jnp.zeros_like(out_ref)

    rep_ref[...] = jnp.dot(
        w_ref[0], e_ref[...], preferred_element_type=jnp.float32
    ).astype(jnp.bfloat16)
    lane = lax.broadcasted_iota(jnp.int32, (GROUP, TILE), 1)
    row = lax.broadcasted_iota(jnp.int32, (GROUP, TILE), 0)
    keep = (lane // SUPPORT) == row
    vrow = lax.broadcasted_iota(jnp.int32, (TILE, TILE), 0)
    urow = lax.broadcasted_iota(jnp.int32, (rows, TILE), 0)
    zero = jnp.zeros((GROUP, TILE), jnp.bfloat16)

    def body(g, carry):
        start = pl.multiple_of(g * GROUP, GROUP)
        blocks = [
            jnp.where(keep, rep_ref[pl.ds(start, GROUP), pl.ds(i * TILE, TILE)], zero)
            for i in range(nblocks)
        ]
        wbd = jnp.concatenate(blocks, axis=0)
        vob = vob_ref[0, pl.ds(g, 1), :]
        cst = (vrow == vob).astype(jnp.bfloat16)
        spread = lax.dot_general(
            wbd, cst, (((1,), (1,)), ((), ())), preferred_element_type=jnp.float32
        ).astype(jnp.bfloat16)
        at = pl.multiple_of(g * depth, depth)
        x_ref[0, pl.ds(at, depth), :] = spread[:depth]
        x_ref[1, pl.ds(at, depth), :] = spread[depth:]
        uoa = uoa_ref[0, pl.ds(g, 1), :]
        r_ref[:, pl.ds(at, TILE)] = (urow == uoa).astype(jnp.bfloat16)
        return carry

    lax.fori_loop(0, ngroups, body, 0, unroll=4)
    pick = r_ref[...]
    out_ref[0] += jnp.dot(pick, x_ref[0], preferred_element_type=jnp.float32)
    out_ref[1] += jnp.dot(pick, x_ref[1], preferred_element_type=jnp.float32)


def grid_rows(weighted, vob, uoa, rows):
    dests, per_dest, width = weighted.shape
    chunk = per_dest
    for size in (384, 192, 96, 48, 16):
        if per_dest % size == 0 and size <= per_dest:
            chunk = size
            break
    steps = per_dest // chunk
    nblocks = width // SUPPORT
    lanes_in = lax.broadcasted_iota(jnp.int32, (width, nblocks * TILE), 0)
    lanes_out = lax.broadcasted_iota(jnp.int32, (width, nblocks * TILE), 1)
    expand = (
        (lanes_in // SUPPORT == lanes_out // TILE) & (lanes_in % SUPPORT == lanes_out % SUPPORT)
    ).astype(jnp.bfloat16)
    return pl.pallas_call(
        grid_kernel,
        grid=(dests, steps),
        in_specs=[
            pl.BlockSpec((1, chunk, width), lambda d, c: (d, c, 0)),
            pl.BlockSpec((1, chunk // GROUP, TILE), lambda d, c: (d, c, 0)),
            pl.BlockSpec((1, chunk // GROUP, TILE), lambda d, c: (d, c, 0)),
            pl.BlockSpec((width, nblocks * TILE), lambda d, c: (0, 0)),
        ],
        out_specs=pl.BlockSpec((2, rows, TILE), lambda d, c: (0, 0, d)),
        out_shape=jax.ShapeDtypeStruct((2, rows, dests * TILE), jnp.float32),
        scratch_shapes=[
            pltpu.VMEM((chunk, nblocks * TILE), jnp.bfloat16),
            pltpu.VMEM((2, chunk * SUPPORT, TILE), jnp.bfloat16),
            pltpu.VMEM((rows, chunk * SUPPORT), jnp.bfloat16),
        ],
        compiler_params=pltpu.CompilerParams(
            dimension_semantics=("arbitrary", "arbitrary")
        ),
    )(weighted, vob, uoa, expand)


def shards(visibilities, tile_counts, w_plane, u_offset, v_offset, kernels):
    dests = visibilities.shape[2]
    ntiles = visibilities.shape[3]
    slots = visibilities.shape[4]
    axes = ("uv", "rep")
    ndev = lax.axis_size(axes)
    rows = ntiles * TILE // ndev
    per_tile = ndev // ntiles
    own_dests = dests // per_tile
    me = lax.axis_index(axes)
    member = me % per_tile
    live = (
        lax.broadcasted_iota(jnp.int32, (dests, ntiles, slots), 2) < tile_counts[0][:, :, None]
    ).astype(jnp.float32)
    fields = jnp.stack(
        [
            visibilities[0, 0] * live,
            visibilities[1, 0] * live,
            w_plane[0].astype(jnp.float32),
            u_offset[0].astype(jnp.float32),
            v_offset[0].astype(jnp.float32),
        ]
    )
    send = fields.reshape(FIELDS, per_tile, own_dests, ntiles, slots).transpose(3, 1, 0, 2, 4)
    send = send.reshape(ndev, FIELDS, own_dests, slots)
    got = lax.all_to_all(send, axes, split_axis=0, concat_axis=0, tiled=True)
    got = got.transpose(1, 2, 0, 3).reshape(FIELDS, own_dests, ndev * slots)
    vis_re = got[0]
    vis_im = got[1]
    planes = got[2].astype(jnp.int32)
    rows_first = got[3].astype(jnp.int32)
    cols_first = got[4].astype(jnp.int32)
    if vis_re.size <= 65536:
        weighted = weigh(vis_re, vis_im, planes, kernels)
    else:
        weighted = lax.map(lambda x: weigh(x[0], x[1], x[2], kernels), (vis_re, vis_im, planes))
    per_dest = ndev * slots
    ngroups = per_dest // GROUP
    taps = jnp.arange(SUPPORT, dtype=jnp.int32)
    vob = (cols_first.reshape(own_dests, ngroups, GROUP, 1) + taps).reshape(own_dests, ngroups, TILE)
    uoa = (rows_first.reshape(own_dests, ngroups, 1, GROUP) + taps[:, None]).reshape(
        own_dests, ngroups, TILE
    )
    slab = grid_rows(weighted, vob, uoa, TILE)
    width = own_dests * TILE
    mine = lax.dynamic_slice_in_dim(slab, member * rows, rows, axis=1)
    full = jnp.zeros((2, rows, dests * TILE), jnp.float32)
    full = lax.dynamic_update_slice_in_dim(full, mine, member * width, axis=2)
    for step in range(1, per_tile):
        target = (member + step) % per_tile
        source = (member + per_tile - step) % per_tile
        pairs = [
            (k, (k // per_tile) * per_tile + (k % per_tile + step) % per_tile)
            for k in range(ndev)
        ]
        piece = lax.dynamic_slice_in_dim(slab, target * rows, rows, axis=1)
        piece = lax.ppermute(piece, axes, pairs)
        full = lax.dynamic_update_slice_in_dim(full, piece, source * width, axis=2)
    return transform(full[0], full[1], dests)


def solution(mesh):
    placed = (
        P(None, ("uv", "rep"), None, None, None),
        P(("uv", "rep"), None, None),
        P(("uv", "rep"), None, None, None),
        P(("uv", "rep"), None, None, None),
        P(("uv", "rep"), None, None, None),
        P(),
    )
    return jax.shard_map(
        shards, mesh=mesh, in_specs=placed, out_specs=P(("uv", "rep"), None, None), check_vma=False
    )
```

```python
import functools
import math

import jax
import jax.numpy as jnp
from jax import lax
from jax.experimental import pallas as pl
from jax.experimental.pallas import tpu as pltpu
from jax.sharding import PartitionSpec as P

TILE = 128
SUPPORT = 8
GROUP = 16
FIELDS = 5


def make_table(first, second, length):
    index_a = lax.broadcasted_iota(jnp.int32, (first, second), 0)
    index_b = lax.broadcasted_iota(jnp.int32, (first, second), 1)
    angle = 2.0 * math.pi / length * (index_a * index_b % length).astype(jnp.float32)
    return (jnp.cos(angle), jnp.sin(angle))


def transform(real_in, imag_in, groups):
    nrows = real_in.shape[0]
    total = real_in.shape[1]
    width = total // groups
    highest = lax.Precision.HIGH
    cos_a, sin_a = make_table(groups, groups, groups)
    cos_t, sin_t = make_table(groups, width, total)
    cos_b, sin_b = make_table(width, width, width)
    real_in = real_in.reshape(nrows, groups, width)
    imag_in = imag_in.reshape(nrows, groups, width)
    first_re = jnp.einsum("rpj,pk->rkj", real_in, cos_a, precision=highest) + jnp.einsum(
        "rpj,pk->rkj", imag_in, sin_a, precision=highest
    )
    first_im = jnp.einsum("rpj,pk->rkj", imag_in, cos_a, precision=highest) - jnp.einsum(
        "rpj,pk->rkj", real_in, sin_a, precision=highest
    )
    turned_re = first_re * cos_t + first_im * sin_t
    turned_im = first_im * cos_t - first_re * sin_t
    final_re = jnp.einsum("rkj,jm->rmk", turned_re, cos_b, precision=highest) + jnp.einsum(
        "rkj,jm->rmk", turned_im, sin_b, precision=highest
    )
    final_im = jnp.einsum("rkj,jm->rmk", turned_im, cos_b, precision=highest) - jnp.einsum(
        "rkj,jm->rmk", turned_re, sin_b, precision=highest
    )
    scale = 1.0 / math.sqrt(total)
    return (
        jnp.stack([final_re.reshape(nrows, total), final_im.reshape(nrows, total)], axis=1) * scale
    )


def weigh(vis_re, vis_im, planes, kernels):
    nplanes = kernels.shape[0]
    width = kernels.shape[1]
    half = width // 2
    onehot = (
        planes[..., None] == lax.broadcasted_iota(jnp.int32, planes.shape + (nplanes,), planes.ndim)
    ).astype(jnp.float32)
    kern = jnp.dot(
        onehot.reshape(-1, nplanes),
        kernels,
        precision=lax.Precision.HIGHEST,
        preferred_element_type=jnp.float32,
    )
    kern = kern.reshape(planes.shape + (width,))
    kern_re = kern[..., :half]
    kern_im = kern[..., half:]
    part_re = vis_re[..., None] * kern_re - vis_im[..., None] * kern_im
    part_im = vis_re[..., None] * kern_im + vis_im[..., None] * kern_re
    return jnp.concatenate([part_re, part_im], axis=-1).astype(jnp.bfloat16)


def grid_kernel(w_ref, vob_ref, uoa_ref, e_ref, out_ref, rep_ref, x_ref, r_ref):
    chunk_step = pl.program_id(1)
    chunk = w_ref.shape[1]
    rows = out_ref.shape[1]
    ngroups = chunk // GROUP
    nblocks = w_ref.shape[2] // SUPPORT
    depth = nblocks * GROUP // 2

    @pl.when(chunk_step == 0)
    def _():
        out_ref[...] = jnp.zeros_like(out_ref)

    rep_ref[...] = jnp.dot(
        w_ref[0], e_ref[...], preferred_element_type=jnp.float32
    ).astype(jnp.bfloat16)
    lane = lax.broadcasted_iota(jnp.int32, (GROUP, TILE), 1)
    row = lax.broadcasted_iota(jnp.int32, (GROUP, TILE), 0)
    keep = (lane // SUPPORT) == row
    vrow = lax.broadcasted_iota(jnp.int32, (TILE, TILE), 0)
    urow = lax.broadcasted_iota(jnp.int32, (rows, TILE), 0)
    zero = jnp.zeros((GROUP, TILE), jnp.bfloat16)

    def body(g, carry):
        start = pl.multiple_of(g * GROUP, GROUP)
        blocks = [
            jnp.where(keep, rep_ref[pl.ds(start, GROUP), pl.ds(i * TILE, TILE)], zero)
            for i in range(nblocks)
        ]
        wbd = jnp.concatenate(blocks, axis=0)
        vob = vob_ref[0, pl.ds(g, 1), :]
        cst = (vrow == vob).astype(jnp.bfloat16)
        spread = lax.dot_general(
            wbd, cst, (((1,), (1,)), ((), ())), preferred_element_type=jnp.float32
        ).astype(jnp.bfloat16)
        at = pl.multiple_of(g * depth, depth)
        x_ref[0, pl.ds(at, depth), :] = spread[:depth]
        x_ref[1, pl.ds(at, depth), :] = spread[depth:]
        uoa = uoa_ref[0, pl.ds(g, 1), :]
        r_ref[:, pl.ds(at, TILE)] = (urow == uoa).astype(jnp.bfloat16)
        return carry

    lax.fori_loop(0, ngroups, body, 0, unroll=4)
    pick = r_ref[...]
    out_ref[0] += jnp.dot(pick, x_ref[0], preferred_element_type=jnp.float32)
    out_ref[1] += jnp.dot(pick, x_ref[1], preferred_element_type=jnp.float32)


def grid_rows(weighted, vob, uoa, rows):
    dests, per_dest, width = weighted.shape
    chunk = per_dest
    for size in (384, 192, 96, 48, 16):
        if per_dest % size == 0 and size <= per_dest:
            chunk = size
            break
    steps = per_dest // chunk
    nblocks = width // SUPPORT
    lanes_in = lax.broadcasted_iota(jnp.int32, (width, nblocks * TILE), 0)
    lanes_out = lax.broadcasted_iota(jnp.int32, (width, nblocks * TILE), 1)
    expand = (
        (lanes_in // SUPPORT == lanes_out // TILE) & (lanes_in % SUPPORT == lanes_out % SUPPORT)
    ).astype(jnp.bfloat16)
    return pl.pallas_call(
        grid_kernel,
        grid=(dests, steps),
        in_specs=[
            pl.BlockSpec((1, chunk, width), lambda d, c: (d, c, 0)),
            pl.BlockSpec((1, chunk // GROUP, TILE), lambda d, c: (d, c, 0)),
            pl.BlockSpec((1, chunk // GROUP, TILE), lambda d, c: (d, c, 0)),
            pl.BlockSpec((width, nblocks * TILE), lambda d, c: (0, 0)),
        ],
        out_specs=pl.BlockSpec((2, rows, TILE), lambda d, c: (0, 0, d)),
        out_shape=jax.ShapeDtypeStruct((2, rows, dests * TILE), jnp.float32),
        scratch_shapes=[
            pltpu.VMEM((chunk, nblocks * TILE), jnp.bfloat16),
            pltpu.VMEM((2, chunk * SUPPORT, TILE), jnp.bfloat16),
            pltpu.VMEM((rows, chunk * SUPPORT), jnp.bfloat16),
        ],
        compiler_params=pltpu.CompilerParams(
            dimension_semantics=("arbitrary", "arbitrary")
        ),
    )(weighted, vob, uoa, expand)


def shards(visibilities, tile_counts, w_plane, u_offset, v_offset, kernels):
    dests = visibilities.shape[2]
    ntiles = visibilities.shape[3]
    slots = visibilities.shape[4]
    axes = ("uv", "rep")
    ndev = lax.axis_size(axes)
    rows = ntiles * TILE // ndev
    per_tile = ndev // ntiles
    own_dests = dests // per_tile
    me = lax.axis_index(axes)
    member = me % per_tile
    live = (
        lax.broadcasted_iota(jnp.int32, (dests, ntiles, slots), 2) < tile_counts[0][:, :, None]
    ).astype(jnp.float32)
    fields = jnp.stack(
        [
            visibilities[0, 0] * live,
            visibilities[1, 0] * live,
            w_plane[0].astype(jnp.float32),
            u_offset[0].astype(jnp.float32),
            v_offset[0].astype(jnp.float32),
        ]
    )
    send = fields.reshape(FIELDS, per_tile, own_dests, ntiles, slots).transpose(3, 1, 0, 2, 4)
    send = send.reshape(ndev, FIELDS, own_dests, slots)
    got = lax.all_to_all(send, axes, split_axis=0, concat_axis=0, tiled=True)
    got = got.transpose(1, 2, 0, 3).reshape(FIELDS, own_dests, ndev * slots)
    vis_re = got[0]
    vis_im = got[1]
    planes = got[2].astype(jnp.int32)
    rows_first = got[3].astype(jnp.int32)
    cols_first = got[4].astype(jnp.int32)
    if vis_re.size <= 65536:
        weighted = weigh(vis_re, vis_im, planes, kernels)
    else:
        weighted = lax.map(lambda x: weigh(x[0], x[1], x[2], kernels), (vis_re, vis_im, planes))
    per_dest = ndev * slots
    ngroups = per_dest // GROUP
    taps = jnp.arange(SUPPORT, dtype=jnp.int32)
    vob = (cols_first.reshape(own_dests, ngroups, GROUP, 1) + taps).reshape(own_dests, ngroups, TILE)
    uoa = (rows_first.reshape(own_dests, ngroups, 1, GROUP) + taps[:, None]).reshape(
        own_dests, ngroups, TILE
    )
    slab = grid_rows(weighted, vob, uoa, TILE)
    width = own_dests * TILE
    mine = lax.dynamic_slice_in_dim(slab, member * rows, rows, axis=1)
    full = jnp.zeros((2, rows, dests * TILE), jnp.float32)
    full = lax.dynamic_update_slice_in_dim(full, mine, member * width, axis=2)
    for step in range(1, per_tile):
        target = (member + step) % per_tile
        source = (member + per_tile - step) % per_tile
        pairs = [
            (k, (k // per_tile) * per_tile + (k % per_tile + step) % per_tile)
            for k in range(ndev)
        ]
        piece = lax.dynamic_slice_in_dim(slab, target * rows, rows, axis=1)
        piece = lax.ppermute(piece, axes, pairs)
        full = lax.dynamic_update_slice_in_dim(full, piece, source * width, axis=2)
    return transform(full[0], full[1], dests)


def solution(mesh):
    placed = (
        P(None, ("uv", "rep"), None, None, None),
        P(("uv", "rep"), None, None),
        P(("uv", "rep"), None, None, None),
        P(("uv", "rep"), None, None, None),
        P(("uv", "rep"), None, None, None),
        P(),
    )
    return jax.shard_map(
        shards, mesh=mesh, in_specs=placed, out_specs=P(("uv", "rep"), None, None), check_vma=False
    )
```

```python
import functools
import math

import jax
import jax.numpy as jnp
from jax import lax
from jax.experimental import pallas as pl
from jax.experimental.pallas import tpu as pltpu
from jax.sharding import PartitionSpec as P

TILE = 128
SUPPORT = 8
GROUP = 16
FIELDS = 5


def make_table(first, second, length):
    index_a = lax.broadcasted_iota(jnp.int32, (first, second), 0)
    index_b = lax.broadcasted_iota(jnp.int32, (first, second), 1)
    angle = 2.0 * math.pi / length * (index_a * index_b % length).astype(jnp.float32)
    return (jnp.cos(angle), jnp.sin(angle))


def transform(real_in, imag_in, groups):
    nrows = real_in.shape[0]
    total = real_in.shape[1]
    width = total // groups
    highest = lax.Precision.HIGH
    cos_a, sin_a = make_table(groups, groups, groups)
    cos_t, sin_t = make_table(groups, width, total)
    cos_b, sin_b = make_table(width, width, width)
    real_in = real_in.reshape(nrows, groups, width)
    imag_in = imag_in.reshape(nrows, groups, width)
    first_re = jnp.einsum("rpj,pk->rkj", real_in, cos_a, precision=highest) + jnp.einsum(
        "rpj,pk->rkj", imag_in, sin_a, precision=highest
    )
    first_im = jnp.einsum("rpj,pk->rkj", imag_in, cos_a, precision=highest) - jnp.einsum(
        "rpj,pk->rkj", real_in, sin_a, precision=highest
    )
    turned_re = first_re * cos_t + first_im * sin_t
    turned_im = first_im * cos_t - first_re * sin_t
    final_re = jnp.einsum("rkj,jm->rmk", turned_re, cos_b, precision=highest) + jnp.einsum(
        "rkj,jm->rmk", turned_im, sin_b, precision=highest
    )
    final_im = jnp.einsum("rkj,jm->rmk", turned_im, cos_b, precision=highest) - jnp.einsum(
        "rkj,jm->rmk", turned_re, sin_b, precision=highest
    )
    scale = 1.0 / math.sqrt(total)
    return (
        jnp.stack([final_re.reshape(nrows, total), final_im.reshape(nrows, total)], axis=1) * scale
    )


def weigh(vis_re, vis_im, planes, kernels):
    nplanes = kernels.shape[0]
    width = kernels.shape[1]
    half = width // 2
    onehot = (
        planes[..., None] == lax.broadcasted_iota(jnp.int32, planes.shape + (nplanes,), planes.ndim)
    ).astype(jnp.float32)
    kern = jnp.dot(
        onehot.reshape(-1, nplanes),
        kernels,
        precision=lax.Precision.HIGHEST,
        preferred_element_type=jnp.float32,
    )
    kern = kern.reshape(planes.shape + (width,))
    kern_re = kern[..., :half]
    kern_im = kern[..., half:]
    part_re = vis_re[..., None] * kern_re - vis_im[..., None] * kern_im
    part_im = vis_re[..., None] * kern_im + vis_im[..., None] * kern_re
    return jnp.concatenate([part_re, part_im], axis=-1).astype(jnp.bfloat16)


def split3(values):
    high = lax.reduce_precision(values, exponent_bits=8, mantissa_bits=7)
    rest = values - high
    middle = lax.reduce_precision(rest, exponent_bits=8, mantissa_bits=7)
    low = rest - middle
    return high.astype(jnp.bfloat16), middle.astype(jnp.bfloat16), low.astype(jnp.bfloat16)


def grid_kernel(fld_ref, eye_ref, kt_ref, xv_ref, xu_ref, e_ref, out_ref, rep_ref, x_ref, r_ref, tab_ref):
    chunk_step = pl.program_id(1)
    chunk = fld_ref.shape[2]
    rows = out_ref.shape[1]
    ngroups = chunk // GROUP
    width = 2 * SUPPORT * SUPPORT
    nblocks = width // SUPPORT
    depth = nblocks * GROUP // 2
    nplanes = kt_ref.shape[0]

    @pl.when(chunk_step == 0)
    def _():
        out_ref[...] = jnp.zeros_like(out_ref)

    fld = fld_ref[0]
    cols = lax.dot_general(
        eye_ref[...], fld, (((1,), (1,)), ((), ())), preferred_element_type=jnp.float32
    )
    nf = fld.shape[0] // 3
    cols = (cols[:, 0:nf] + cols[:, nf:2 * nf]) + cols[:, 2 * nf:3 * nf]
    vis_re = cols[:, 0:1]
    vis_im = cols[:, 1:2]
    planes = cols[:, 2:3].astype(jnp.int32)
    onehot = (planes == lax.broadcasted_iota(jnp.int32, (chunk, nplanes), 1)).astype(jnp.bfloat16)
    parts = jnp.dot(onehot, kt_ref[...], preferred_element_type=jnp.float32)
    kern_a = (parts[:, 0:width] + parts[:, width:2 * width]) + parts[:, 2 * width:3 * width]
    kern_b = (parts[:, 3 * width:4 * width] + parts[:, 4 * width:5 * width]) + parts[:, 5 * width:6 * width]
    lane = lax.broadcasted_iota(jnp.int32, (chunk, width), 1)
    signed_im = jnp.where(lane < width // 2, -vis_im, vis_im)
    weighted = (vis_re * kern_a + signed_im * kern_b).astype(jnp.bfloat16)

    gmask = (
        lax.broadcasted_iota(jnp.int32, (ngroups, chunk), 1) // GROUP
        == lax.broadcasted_iota(jnp.int32, (ngroups, chunk), 0)
    )
    zero_row = jnp.zeros((ngroups, chunk), jnp.bfloat16)
    vo_rows = jnp.where(gmask, fld[4:5, :], zero_row)
    uo_rows = jnp.where(gmask, fld[3:4, :], zero_row)
    tlane = lax.broadcasted_iota(jnp.int32, (ngroups, TILE), 1)
    tab_ref[0] = jnp.dot(vo_rows, xv_ref[...], preferred_element_type=jnp.float32).astype(jnp.int32) + tlane % SUPPORT
    tab_ref[1] = jnp.dot(uo_rows, xu_ref[...], preferred_element_type=jnp.float32).astype(jnp.int32) + tlane // GROUP

    rep_ref[...] = jnp.dot(
        weighted, e_ref[...], preferred_element_type=jnp.float32
    ).astype(jnp.bfloat16)
    lane = lax.broadcasted_iota(jnp.int32, (GROUP, TILE), 1)
    row = lax.broadcasted_iota(jnp.int32, (GROUP, TILE), 0)
    keep = (lane // SUPPORT) == row
    vrow = lax.broadcasted_iota(jnp.int32, (TILE, TILE), 0)
    urow = lax.broadcasted_iota(jnp.int32, (rows, TILE), 0)
    zero = jnp.zeros((GROUP, TILE), jnp.bfloat16)

    def body(g, carry):
        start = pl.multiple_of(g * GROUP, GROUP)
        blocks = [
            jnp.where(keep, rep_ref[pl.ds(start, GROUP), pl.ds(i * TILE, TILE)], zero)
            for i in range(nblocks)
        ]
        wbd = jnp.concatenate(blocks, axis=0)
        vob = tab_ref[0, pl.ds(g, 1), :]
        cst = (vrow == vob).astype(jnp.bfloat16)
        spread = lax.dot_general(
            wbd, cst, (((1,), (1,)), ((), ())), preferred_element_type=jnp.float32
        ).astype(jnp.bfloat16)
        at = pl.multiple_of(g * depth, depth)
        x_ref[0, pl.ds(at, depth), :] = spread[:depth]
        x_ref[1, pl.ds(at, depth), :] = spread[depth:]
        uoa = tab_ref[1, pl.ds(g, 1), :]
        r_ref[:, pl.ds(at, TILE)] = (urow == uoa).astype(jnp.bfloat16)
        return carry

    lax.fori_loop(0, ngroups, body, 0, unroll=4)
    pick = r_ref[...]
    out_ref[0] += jnp.dot(pick, x_ref[0], preferred_element_type=jnp.float32)
    out_ref[1] += jnp.dot(pick, x_ref[1], preferred_element_type=jnp.float32)


def grid_rows(fld, kernels, rows):
    dests, nf, per_dest = fld.shape
    chunk = per_dest
    for size in (384, 192, 96, 48, 16):
        if per_dest % size == 0 and size <= per_dest:
            chunk = size
            break
    steps = per_dest // chunk
    ngroups = chunk // GROUP
    width = kernels.shape[1]
    half = width // 2
    nblocks = width // SUPPORT
    lanes_in = lax.broadcasted_iota(jnp.int32, (width, nblocks * TILE), 0)
    lanes_out = lax.broadcasted_iota(jnp.int32, (width, nblocks * TILE), 1)
    expand = (
        (lanes_in // SUPPORT == lanes_out // TILE) & (lanes_in % SUPPORT == lanes_out % SUPPORT)
    ).astype(jnp.bfloat16)
    eye = (
        lax.broadcasted_iota(jnp.int32, (chunk, chunk), 0)
        == lax.broadcasted_iota(jnp.int32, (chunk, chunk), 1)
    ).astype(jnp.bfloat16)
    swapped = jnp.concatenate([kernels[:, half:], kernels[:, :half]], axis=1)
    table = jnp.concatenate(split3(kernels) + split3(swapped), axis=1)
    n_in = lax.broadcasted_iota(jnp.int32, (chunk, TILE), 0) % GROUP
    lane_t = lax.broadcasted_iota(jnp.int32, (chunk, TILE), 1)
    expand_v = (n_in == lane_t // SUPPORT).astype(jnp.bfloat16)
    expand_u = (n_in == lane_t % GROUP).astype(jnp.bfloat16)
    whole = lambda d, c: (0, 0)
    return pl.pallas_call(
        grid_kernel,
        grid=(dests, steps),
        in_specs=[
            pl.BlockSpec((1, nf, chunk), lambda d, c: (d, 0, c)),
            pl.BlockSpec((chunk, chunk), whole),
            pl.BlockSpec(table.shape, whole),
            pl.BlockSpec((chunk, TILE), whole),
            pl.BlockSpec((chunk, TILE), whole),
            pl.BlockSpec((width, nblocks * TILE), whole),
        ],
        out_specs=pl.BlockSpec((2, rows, TILE), lambda d, c: (0, 0, d)),
        out_shape=jax.ShapeDtypeStruct((2, rows, dests * TILE), jnp.float32),
        scratch_shapes=[
            pltpu.VMEM((chunk, nblocks * TILE), jnp.bfloat16),
            pltpu.VMEM((2, chunk * SUPPORT, TILE), jnp.bfloat16),
            pltpu.VMEM((rows, chunk * SUPPORT), jnp.bfloat16),
            pltpu.VMEM((2, ngroups, TILE), jnp.int32),
        ],
        compiler_params=pltpu.CompilerParams(
            dimension_semantics=("arbitrary", "arbitrary")
        ),
    )(fld, eye, table, expand_v, expand_u, expand)


def shards(visibilities, tile_counts, w_plane, u_offset, v_offset, kernels):
    dests = visibilities.shape[2]
    ntiles = visibilities.shape[3]
    slots = visibilities.shape[4]
    axes = ("uv", "rep")
    ndev = lax.axis_size(axes)
    rows = ntiles * TILE // ndev
    per_tile = ndev // ntiles
    own_dests = dests // per_tile
    me = lax.axis_index(axes)
    member = me % per_tile
    live = (
        lax.broadcasted_iota(jnp.int32, (dests, ntiles, slots), 2) < tile_counts[0][:, :, None]
    ).astype(jnp.float32)
    fields = jnp.stack(
        [
            visibilities[0, 0] * live,
            visibilities[1, 0] * live,
            w_plane[0].astype(jnp.float32),
            u_offset[0].astype(jnp.float32),
            v_offset[0].astype(jnp.float32),
        ]
    )
    send = fields.reshape(FIELDS, per_tile, own_dests, ntiles, slots).transpose(3, 1, 0, 2, 4)
    send = send.reshape(ndev, FIELDS, own_dests, slots)
    got = lax.all_to_all(send, axes, split_axis=0, concat_axis=0, tiled=True)
    got = got.transpose(1, 2, 0, 3).reshape(FIELDS, own_dests, ndev * slots)
    got = jnp.pad(got.transpose(1, 0, 2), ((0, 0), (0, 8 - FIELDS), (0, 0)))
    got = jnp.concatenate(split3(got), axis=1)
    slab = grid_rows(got, kernels, TILE)
    width = own_dests * TILE
    mine = lax.dynamic_slice_in_dim(slab, member * rows, rows, axis=1)
    full = jnp.zeros((2, rows, dests * TILE), jnp.float32)
    full = lax.dynamic_update_slice_in_dim(full, mine, member * width, axis=2)
    for step in range(1, per_tile):
        target = (member + step) % per_tile
        source = (member + per_tile - step) % per_tile
        pairs = [
            (k, (k // per_tile) * per_tile + (k % per_tile + step) % per_tile)
            for k in range(ndev)
        ]
        piece = lax.dynamic_slice_in_dim(slab, target * rows, rows, axis=1)
        piece = lax.ppermute(piece, axes, pairs)
        full = lax.dynamic_update_slice_in_dim(full, piece, source * width, axis=2)
    return transform(full[0], full[1], dests)


def solution(mesh):
    placed = (
        P(None, ("uv", "rep"), None, None, None),
        P(("uv", "rep"), None, None),
        P(("uv", "rep"), None, None, None),
        P(("uv", "rep"), None, None, None),
        P(("uv", "rep"), None, None, None),
        P(),
    )
    return jax.shard_map(
        shards, mesh=mesh, in_specs=placed, out_specs=P(("uv", "rep"), None, None), check_vma=False
    )
```

```python
import functools
import math

import jax
import jax.numpy as jnp
from jax import lax
from jax.experimental import pallas as pl
from jax.experimental.pallas import tpu as pltpu
from jax.sharding import PartitionSpec as P

TILE = 128
SUPPORT = 8
GROUP = 16
FIELDS = 5


def make_table(first, second, length):
    index_a = lax.broadcasted_iota(jnp.int32, (first, second), 0)
    index_b = lax.broadcasted_iota(jnp.int32, (first, second), 1)
    angle = 2.0 * math.pi / length * (index_a * index_b % length).astype(jnp.float32)
    return (jnp.cos(angle), jnp.sin(angle))


def transform(real_in, imag_in, groups):
    nrows = real_in.shape[0]
    total = real_in.shape[1]
    width = total // groups
    highest = lax.Precision.HIGH
    cos_a, sin_a = make_table(groups, groups, groups)
    cos_t, sin_t = make_table(groups, width, total)
    cos_b, sin_b = make_table(width, width, width)
    real_in = real_in.reshape(nrows, groups, width)
    imag_in = imag_in.reshape(nrows, groups, width)
    first_re = jnp.einsum("rpj,pk->rkj", real_in, cos_a, precision=highest) + jnp.einsum(
        "rpj,pk->rkj", imag_in, sin_a, precision=highest
    )
    first_im = jnp.einsum("rpj,pk->rkj", imag_in, cos_a, precision=highest) - jnp.einsum(
        "rpj,pk->rkj", real_in, sin_a, precision=highest
    )
    turned_re = first_re * cos_t + first_im * sin_t
    turned_im = first_im * cos_t - first_re * sin_t
    final_re = jnp.einsum("rkj,jm->rmk", turned_re, cos_b, precision=highest) + jnp.einsum(
        "rkj,jm->rmk", turned_im, sin_b, precision=highest
    )
    final_im = jnp.einsum("rkj,jm->rmk", turned_im, cos_b, precision=highest) - jnp.einsum(
        "rkj,jm->rmk", turned_re, sin_b, precision=highest
    )
    scale = 1.0 / math.sqrt(total)
    return (
        jnp.stack([final_re.reshape(nrows, total), final_im.reshape(nrows, total)], axis=1) * scale
    )


def weigh(vis_re, vis_im, planes, kernels):
    nplanes = kernels.shape[0]
    width = kernels.shape[1]
    half = width // 2
    onehot = (
        planes[..., None] == lax.broadcasted_iota(jnp.int32, planes.shape + (nplanes,), planes.ndim)
    ).astype(jnp.float32)
    kern = jnp.dot(
        onehot.reshape(-1, nplanes),
        kernels,
        precision=lax.Precision.HIGHEST,
        preferred_element_type=jnp.float32,
    )
    kern = kern.reshape(planes.shape + (width,))
    kern_re = kern[..., :half]
    kern_im = kern[..., half:]
    part_re = vis_re[..., None] * kern_re - vis_im[..., None] * kern_im
    part_im = vis_re[..., None] * kern_im + vis_im[..., None] * kern_re
    return jnp.concatenate([part_re, part_im], axis=-1).astype(jnp.bfloat16)


def split3(values):
    high = lax.reduce_precision(values, exponent_bits=8, mantissa_bits=7)
    rest = values - high
    middle = lax.reduce_precision(rest, exponent_bits=8, mantissa_bits=7)
    low = rest - middle
    return high.astype(jnp.bfloat16), middle.astype(jnp.bfloat16), low.astype(jnp.bfloat16)


def grid_kernel(fld_ref, eye_ref, kt_ref, xv_ref, xu_ref, e_ref, out_ref, rep_ref, x_ref, r_ref, tab_ref):
    chunk_step = pl.program_id(1)
    chunk = fld_ref.shape[2]
    rows = out_ref.shape[1]
    ngroups = chunk // GROUP
    width = 2 * SUPPORT * SUPPORT
    nblocks = width // SUPPORT
    depth = nblocks * GROUP // 2
    nplanes = kt_ref.shape[0]

    @pl.when(chunk_step == 0)
    def _():
        out_ref[...] = jnp.zeros_like(out_ref)

    fld = fld_ref[0]
    cols = lax.dot_general(
        eye_ref[...], fld, (((1,), (1,)), ((), ())), preferred_element_type=jnp.float32
    )
    nf = fld.shape[0] // 3
    cols = (cols[:, 0:nf] + cols[:, nf:2 * nf]) + cols[:, 2 * nf:3 * nf]
    vis_re = cols[:, 0:1]
    vis_im = cols[:, 1:2]
    planes = cols[:, 2:3].astype(jnp.int32)
    onehot = (planes == lax.broadcasted_iota(jnp.int32, (chunk, nplanes), 1)).astype(jnp.bfloat16)
    parts = jnp.dot(onehot, kt_ref[...], preferred_element_type=jnp.float32)
    kern_a = (parts[:, 0:width] + parts[:, width:2 * width]) + parts[:, 2 * width:3 * width]
    kern_b = (parts[:, 3 * width:4 * width] + parts[:, 4 * width:5 * width]) + parts[:, 5 * width:6 * width]
    lane = lax.broadcasted_iota(jnp.int32, (chunk, width), 1)
    signed_im = jnp.where(lane < width // 2, -vis_im, vis_im)
    weighted = (vis_re * kern_a + signed_im * kern_b).astype(jnp.bfloat16)

    gmask = (
        lax.broadcasted_iota(jnp.int32, (ngroups, chunk), 1) // GROUP
        == lax.broadcasted_iota(jnp.int32, (ngroups, chunk), 0)
    )
    zero_row = jnp.zeros((ngroups, chunk), jnp.bfloat16)
    vo_rows = jnp.where(gmask, fld[4:5, :], zero_row)
    uo_rows = jnp.where(gmask, fld[3:4, :], zero_row)
    tlane = lax.broadcasted_iota(jnp.int32, (ngroups, TILE), 1)
    tab_ref[0] = jnp.dot(vo_rows, xv_ref[...], preferred_element_type=jnp.float32).astype(jnp.int32) + tlane % SUPPORT
    tab_ref[1] = jnp.dot(uo_rows, xu_ref[...], preferred_element_type=jnp.float32).astype(jnp.int32) + tlane // GROUP

    rep_ref[...] = jnp.dot(
        weighted, e_ref[...], preferred_element_type=jnp.float32
    ).astype(jnp.bfloat16)
    lane = lax.broadcasted_iota(jnp.int32, (GROUP, TILE), 1)
    row = lax.broadcasted_iota(jnp.int32, (GROUP, TILE), 0)
    keep = (lane // SUPPORT) == row
    vrow = lax.broadcasted_iota(jnp.int32, (TILE, TILE), 0)
    urow = lax.broadcasted_iota(jnp.int32, (rows, TILE), 0)
    zero = jnp.zeros((GROUP, TILE), jnp.bfloat16)

    def body(g, carry):
        start = pl.multiple_of(g * GROUP, GROUP)
        blocks = [
            jnp.where(keep, rep_ref[pl.ds(start, GROUP), pl.ds(i * TILE, TILE)], zero)
            for i in range(nblocks)
        ]
        wbd = jnp.concatenate(blocks, axis=0)
        vob = tab_ref[0, pl.ds(g, 1), :]
        cst = (vrow == vob).astype(jnp.bfloat16)
        spread = lax.dot_general(
            wbd, cst, (((1,), (1,)), ((), ())), preferred_element_type=jnp.float32
        ).astype(jnp.bfloat16)
        at = pl.multiple_of(g * depth, depth)
        x_ref[0, pl.ds(at, depth), :] = spread[:depth]
        x_ref[1, pl.ds(at, depth), :] = spread[depth:]
        uoa = tab_ref[1, pl.ds(g, 1), :]
        r_ref[:, pl.ds(at, TILE)] = (urow == uoa).astype(jnp.bfloat16)
        return carry

    lax.fori_loop(0, ngroups, body, 0, unroll=True)
    pick = r_ref[...]
    out_ref[0] += jnp.dot(pick, x_ref[0], preferred_element_type=jnp.float32)
    out_ref[1] += jnp.dot(pick, x_ref[1], preferred_element_type=jnp.float32)


def grid_rows(fld, kernels, rows):
    dests, nf, per_dest = fld.shape
    chunk = per_dest
    for size in (384, 192, 96, 48, 16):
        if per_dest % size == 0 and size <= per_dest:
            chunk = size
            break
    steps = per_dest // chunk
    ngroups = chunk // GROUP
    width = kernels.shape[1]
    half = width // 2
    nblocks = width // SUPPORT
    lanes_in = lax.broadcasted_iota(jnp.int32, (width, nblocks * TILE), 0)
    lanes_out = lax.broadcasted_iota(jnp.int32, (width, nblocks * TILE), 1)
    expand = (
        (lanes_in // SUPPORT == lanes_out // TILE) & (lanes_in % SUPPORT == lanes_out % SUPPORT)
    ).astype(jnp.bfloat16)
    eye = (
        lax.broadcasted_iota(jnp.int32, (chunk, chunk), 0)
        == lax.broadcasted_iota(jnp.int32, (chunk, chunk), 1)
    ).astype(jnp.bfloat16)
    swapped = jnp.concatenate([kernels[:, half:], kernels[:, :half]], axis=1)
    table = jnp.concatenate(split3(kernels) + split3(swapped), axis=1)
    n_in = lax.broadcasted_iota(jnp.int32, (chunk, TILE), 0) % GROUP
    lane_t = lax.broadcasted_iota(jnp.int32, (chunk, TILE), 1)
    expand_v = (n_in == lane_t // SUPPORT).astype(jnp.bfloat16)
    expand_u = (n_in == lane_t % GROUP).astype(jnp.bfloat16)
    whole = lambda d, c: (0, 0)
    return pl.pallas_call(
        grid_kernel,
        grid=(dests, steps),
        in_specs=[
            pl.BlockSpec((1, nf, chunk), lambda d, c: (d, 0, c)),
            pl.BlockSpec((chunk, chunk), whole),
            pl.BlockSpec(table.shape, whole),
            pl.BlockSpec((chunk, TILE), whole),
            pl.BlockSpec((chunk, TILE), whole),
            pl.BlockSpec((width, nblocks * TILE), whole),
        ],
        out_specs=pl.BlockSpec((2, rows, TILE), lambda d, c: (0, 0, d)),
        out_shape=jax.ShapeDtypeStruct((2, rows, dests * TILE), jnp.float32),
        scratch_shapes=[
            pltpu.VMEM((chunk, nblocks * TILE), jnp.bfloat16),
            pltpu.VMEM((2, chunk * SUPPORT, TILE), jnp.bfloat16),
            pltpu.VMEM((rows, chunk * SUPPORT), jnp.bfloat16),
            pltpu.VMEM((2, ngroups, TILE), jnp.int32),
        ],
        compiler_params=pltpu.CompilerParams(
            dimension_semantics=("arbitrary", "arbitrary")
        ),
    )(fld, eye, table, expand_v, expand_u, expand)


def shards(visibilities, tile_counts, w_plane, u_offset, v_offset, kernels):
    dests = visibilities.shape[2]
    ntiles = visibilities.shape[3]
    slots = visibilities.shape[4]
    axes = ("uv", "rep")
    ndev = lax.axis_size(axes)
    rows = ntiles * TILE // ndev
    per_tile = ndev // ntiles
    own_dests = dests // per_tile
    me = lax.axis_index(axes)
    member = me % per_tile
    live = (
        lax.broadcasted_iota(jnp.int32, (dests, ntiles, slots), 2) < tile_counts[0][:, :, None]
    ).astype(jnp.float32)
    fields = jnp.stack(
        [
            visibilities[0, 0] * live,
            visibilities[1, 0] * live,
            w_plane[0].astype(jnp.float32),
            u_offset[0].astype(jnp.float32),
            v_offset[0].astype(jnp.float32),
        ]
    )
    send = fields.reshape(FIELDS, per_tile, own_dests, ntiles, slots).transpose(3, 1, 0, 2, 4)
    send = send.reshape(ndev, FIELDS, own_dests, slots)
    got = lax.all_to_all(send, axes, split_axis=0, concat_axis=0, tiled=True)
    got = got.transpose(1, 2, 0, 3).reshape(FIELDS, own_dests, ndev * slots)
    got = jnp.pad(got.transpose(1, 0, 2), ((0, 0), (0, 8 - FIELDS), (0, 0)))
    got = jnp.concatenate(split3(got), axis=1)
    slab = grid_rows(got, kernels, TILE)
    width = own_dests * TILE
    mine = lax.dynamic_slice_in_dim(slab, member * rows, rows, axis=1)
    full = jnp.zeros((2, rows, dests * TILE), jnp.float32)
    full = lax.dynamic_update_slice_in_dim(full, mine, member * width, axis=2)
    for step in range(1, per_tile):
        target = (member + step) % per_tile
        source = (member + per_tile - step) % per_tile
        pairs = [
            (k, (k // per_tile) * per_tile + (k % per_tile + step) % per_tile)
            for k in range(ndev)
        ]
        piece = lax.dynamic_slice_in_dim(slab, target * rows, rows, axis=1)
        piece = lax.ppermute(piece, axes, pairs)
        full = lax.dynamic_update_slice_in_dim(full, piece, source * width, axis=2)
    return transform(full[0], full[1], dests)


def solution(mesh):
    placed = (
        P(None, ("uv", "rep"), None, None, None),
        P(("uv", "rep"), None, None),
        P(("uv", "rep"), None, None, None),
        P(("uv", "rep"), None, None, None),
        P(("uv", "rep"), None, None, None),
        P(),
    )
    return jax.shard_map(
        shards, mesh=mesh, in_specs=placed, out_specs=P(("uv", "rep"), None, None), check_vma=False
    )
```

```python
import functools
import math

import jax
import jax.numpy as jnp
from jax import lax
from jax.experimental import pallas as pl
from jax.experimental.pallas import tpu as pltpu
from jax.sharding import PartitionSpec as P

TILE = 128
SUPPORT = 8
GROUP = 16
FIELDS = 5


def make_table(first, second, length):
    index_a = lax.broadcasted_iota(jnp.int32, (first, second), 0)
    index_b = lax.broadcasted_iota(jnp.int32, (first, second), 1)
    angle = 2.0 * math.pi / length * (index_a * index_b % length).astype(jnp.float32)
    return (jnp.cos(angle), jnp.sin(angle))


def transform(real_in, imag_in, groups):
    nrows = real_in.shape[0]
    total = real_in.shape[1]
    width = total // groups
    highest = lax.Precision.HIGH
    cos_a, sin_a = make_table(groups, groups, groups)
    cos_t, sin_t = make_table(groups, width, total)
    cos_b, sin_b = make_table(width, width, width)
    real_in = real_in.reshape(nrows, groups, width)
    imag_in = imag_in.reshape(nrows, groups, width)
    first_re = jnp.einsum("rpj,pk->rkj", real_in, cos_a, precision=highest) + jnp.einsum(
        "rpj,pk->rkj", imag_in, sin_a, precision=highest
    )
    first_im = jnp.einsum("rpj,pk->rkj", imag_in, cos_a, precision=highest) - jnp.einsum(
        "rpj,pk->rkj", real_in, sin_a, precision=highest
    )
    turned_re = first_re * cos_t + first_im * sin_t
    turned_im = first_im * cos_t - first_re * sin_t
    final_re = jnp.einsum("rkj,jm->rmk", turned_re, cos_b, precision=highest) + jnp.einsum(
        "rkj,jm->rmk", turned_im, sin_b, precision=highest
    )
    final_im = jnp.einsum("rkj,jm->rmk", turned_im, cos_b, precision=highest) - jnp.einsum(
        "rkj,jm->rmk", turned_re, sin_b, precision=highest
    )
    scale = 1.0 / math.sqrt(total)
    return (
        jnp.stack([final_re.reshape(nrows, total), final_im.reshape(nrows, total)], axis=1) * scale
    )


def weigh(vis_re, vis_im, planes, kernels):
    nplanes = kernels.shape[0]
    width = kernels.shape[1]
    half = width // 2
    onehot = (
        planes[..., None] == lax.broadcasted_iota(jnp.int32, planes.shape + (nplanes,), planes.ndim)
    ).astype(jnp.float32)
    kern = jnp.dot(
        onehot.reshape(-1, nplanes),
        kernels,
        precision=lax.Precision.HIGHEST,
        preferred_element_type=jnp.float32,
    )
    kern = kern.reshape(planes.shape + (width,))
    kern_re = kern[..., :half]
    kern_im = kern[..., half:]
    part_re = vis_re[..., None] * kern_re - vis_im[..., None] * kern_im
    part_im = vis_re[..., None] * kern_im + vis_im[..., None] * kern_re
    return jnp.concatenate([part_re, part_im], axis=-1).astype(jnp.bfloat16)


def split3(values):
    high = lax.reduce_precision(values, exponent_bits=8, mantissa_bits=7)
    rest = values - high
    middle = lax.reduce_precision(rest, exponent_bits=8, mantissa_bits=7)
    low = rest - middle
    return high.astype(jnp.bfloat16), middle.astype(jnp.bfloat16), low.astype(jnp.bfloat16)


def grid_kernel(fld_ref, eye_ref, kt_ref, xv_ref, xu_ref, e_ref, out_ref, rep_ref, x_ref, r_ref, tab_ref):
    chunk_step = pl.program_id(1)
    chunk = fld_ref.shape[2]
    rows = out_ref.shape[1]
    ngroups = chunk // GROUP
    width = 2 * SUPPORT * SUPPORT
    nblocks = width // SUPPORT
    depth = nblocks * GROUP // 2
    nplanes = kt_ref.shape[0]

    @pl.when(chunk_step == 0)
    def _():
        out_ref[...] = jnp.zeros_like(out_ref)

    fld = fld_ref[0]
    cols = lax.dot_general(
        eye_ref[...], fld, (((1,), (1,)), ((), ())), preferred_element_type=jnp.float32
    )
    nf = fld.shape[0] // 3
    cols = (cols[:, 0:nf] + cols[:, nf:2 * nf]) + cols[:, 2 * nf:3 * nf]
    vis_re = cols[:, 0:1]
    vis_im = cols[:, 1:2]
    planes = cols[:, 2:3].astype(jnp.int32)
    onehot = (planes == lax.broadcasted_iota(jnp.int32, (chunk, nplanes), 1)).astype(jnp.bfloat16)
    parts = jnp.dot(onehot, kt_ref[...], preferred_element_type=jnp.float32)
    kern_a = (parts[:, 0:width] + parts[:, width:2 * width]) + parts[:, 2 * width:3 * width]
    kern_b = (parts[:, 3 * width:4 * width] + parts[:, 4 * width:5 * width]) + parts[:, 5 * width:6 * width]
    lane = lax.broadcasted_iota(jnp.int32, (chunk, width), 1)
    signed_im = jnp.where(lane < width // 2, -vis_im, vis_im)
    weighted = (vis_re * kern_a + signed_im * kern_b).astype(jnp.bfloat16)

    gmask = (
        lax.broadcasted_iota(jnp.int32, (ngroups, chunk), 1) // GROUP
        == lax.broadcasted_iota(jnp.int32, (ngroups, chunk), 0)
    )
    zero_row = jnp.zeros((ngroups, chunk), jnp.bfloat16)
    vo_rows = jnp.where(gmask, fld[4:5, :], zero_row)
    uo_rows = jnp.where(gmask, fld[3:4, :], zero_row)
    tlane = lax.broadcasted_iota(jnp.int32, (ngroups, TILE), 1)
    tab_ref[0] = jnp.dot(vo_rows, xv_ref[...], preferred_element_type=jnp.float32).astype(jnp.int32) + tlane % SUPPORT
    tab_ref[1] = jnp.dot(uo_rows, xu_ref[...], preferred_element_type=jnp.float32).astype(jnp.int32) + tlane // GROUP

    rep_ref[...] = jnp.dot(
        weighted, e_ref[...], preferred_element_type=jnp.float32
    ).astype(jnp.bfloat16)
    lane = lax.broadcasted_iota(jnp.int32, (GROUP, TILE), 1)
    row = lax.broadcasted_iota(jnp.int32, (GROUP, TILE), 0)
    keep = (lane // SUPPORT) == row
    vrow = lax.broadcasted_iota(jnp.int32, (TILE, TILE), 0)
    urow = lax.broadcasted_iota(jnp.int32, (rows, TILE), 0)
    zero = jnp.zeros((GROUP, TILE), jnp.bfloat16)

    def body(g, carry):
        start = pl.multiple_of(g * GROUP, GROUP)
        blocks = [
            jnp.where(keep, rep_ref[pl.ds(start, GROUP), pl.ds(i * TILE, TILE)], zero)
            for i in range(nblocks)
        ]
        wbd = jnp.concatenate(blocks, axis=0)
        vob = tab_ref[0, pl.ds(g, 1), :]
        cst = (vrow == vob).astype(jnp.bfloat16)
        spread = lax.dot_general(
            wbd, cst, (((1,), (1,)), ((), ())), preferred_element_type=jnp.float32
        ).astype(jnp.bfloat16)
        at = pl.multiple_of(g * depth, depth)
        x_ref[0, pl.ds(at, depth), :] = spread[:depth]
        x_ref[1, pl.ds(at, depth), :] = spread[depth:]
        uoa = tab_ref[1, pl.ds(g, 1), :]
        r_ref[:, pl.ds(at, TILE)] = (urow == uoa).astype(jnp.bfloat16)
        return carry

    lax.fori_loop(0, ngroups, body, 0, unroll=True)
    pick = r_ref[...]
    out_ref[0] += jnp.dot(pick, x_ref[0], preferred_element_type=jnp.float32)
    out_ref[1] += jnp.dot(pick, x_ref[1], preferred_element_type=jnp.float32)


def grid_rows(fld, kernels, rows):
    dests, nf, per_dest = fld.shape
    chunk = per_dest
    for size in (384, 192, 96, 48, 16):
        if per_dest % size == 0 and size <= per_dest:
            chunk = size
            break
    steps = per_dest // chunk
    ngroups = chunk // GROUP
    width = kernels.shape[1]
    half = width // 2
    nblocks = width // SUPPORT
    lanes_in = lax.broadcasted_iota(jnp.int32, (width, nblocks * TILE), 0)
    lanes_out = lax.broadcasted_iota(jnp.int32, (width, nblocks * TILE), 1)
    expand = (
        (lanes_in // SUPPORT == lanes_out // TILE) & (lanes_in % SUPPORT == lanes_out % SUPPORT)
    ).astype(jnp.bfloat16)
    eye = (
        lax.broadcasted_iota(jnp.int32, (chunk, chunk), 0)
        == lax.broadcasted_iota(jnp.int32, (chunk, chunk), 1)
    ).astype(jnp.bfloat16)
    swapped = jnp.concatenate([kernels[:, half:], kernels[:, :half]], axis=1)
    table = jnp.concatenate(split3(kernels) + split3(swapped), axis=1)
    n_in = lax.broadcasted_iota(jnp.int32, (chunk, TILE), 0) % GROUP
    lane_t = lax.broadcasted_iota(jnp.int32, (chunk, TILE), 1)
    expand_v = (n_in == lane_t // SUPPORT).astype(jnp.bfloat16)
    expand_u = (n_in == lane_t % GROUP).astype(jnp.bfloat16)
    whole = lambda d, c: (0, 0)
    return pl.pallas_call(
        grid_kernel,
        grid=(dests, steps),
        in_specs=[
            pl.BlockSpec((1, nf, chunk), lambda d, c: (d, 0, c)),
            pl.BlockSpec((chunk, chunk), whole),
            pl.BlockSpec(table.shape, whole),
            pl.BlockSpec((chunk, TILE), whole),
            pl.BlockSpec((chunk, TILE), whole),
            pl.BlockSpec((width, nblocks * TILE), whole),
        ],
        out_specs=pl.BlockSpec((2, rows, TILE), lambda d, c: (0, 0, d)),
        out_shape=jax.ShapeDtypeStruct((2, rows, dests * TILE), jnp.float32),
        scratch_shapes=[
            pltpu.VMEM((chunk, nblocks * TILE), jnp.bfloat16),
            pltpu.VMEM((2, chunk * SUPPORT, TILE), jnp.bfloat16),
            pltpu.VMEM((rows, chunk * SUPPORT), jnp.bfloat16),
            pltpu.VMEM((2, ngroups, TILE), jnp.int32),
        ],
        compiler_params=pltpu.CompilerParams(
            dimension_semantics=("arbitrary", "arbitrary")
        ),
    )(fld, eye, table, expand_v, expand_u, expand)


def shards(visibilities, tile_counts, w_plane, u_offset, v_offset, kernels):
    dests = visibilities.shape[2]
    ntiles = visibilities.shape[3]
    slots = visibilities.shape[4]
    axes = ("uv", "rep")
    ndev = lax.axis_size(axes)
    rows = ntiles * TILE // ndev
    per_tile = ndev // ntiles
    own_dests = dests // per_tile
    me = lax.axis_index(axes)
    member = me % per_tile
    live = (
        lax.broadcasted_iota(jnp.int32, (dests, ntiles, slots), 2) < tile_counts[0][:, :, None]
    ).astype(jnp.float32)
    fields = jnp.concatenate(
        [
            visibilities[0, 0] * live,
            visibilities[1, 0] * live,
            w_plane[0].astype(jnp.float32),
            u_offset[0].astype(jnp.float32),
            v_offset[0].astype(jnp.float32),
        ],
        axis=-1,
    )
    send = fields.reshape(per_tile, own_dests, ntiles, FIELDS * slots).transpose(2, 0, 1, 3)
    send = send.reshape(ndev, own_dests * FIELDS * slots)
    got = lax.all_to_all(send, axes, split_axis=0, concat_axis=0, tiled=True)
    got = got.reshape(ndev, own_dests, FIELDS, slots).transpose(1, 2, 0, 3)
    got = got.reshape(own_dests, FIELDS, ndev * slots)
    got = jnp.pad(got, ((0, 0), (0, 8 - FIELDS), (0, 0)))
    got = jnp.concatenate(split3(got), axis=1)
    slab = grid_rows(got, kernels, TILE)
    width = own_dests * TILE
    mine = lax.dynamic_slice_in_dim(slab, member * rows, rows, axis=1)
    full = jnp.zeros((2, rows, dests * TILE), jnp.float32)
    full = lax.dynamic_update_slice_in_dim(full, mine, member * width, axis=2)
    for step in range(1, per_tile):
        target = (member + step) % per_tile
        source = (member + per_tile - step) % per_tile
        pairs = [
            (k, (k // per_tile) * per_tile + (k % per_tile + step) % per_tile)
            for k in range(ndev)
        ]
        piece = lax.dynamic_slice_in_dim(slab, target * rows, rows, axis=1)
        piece = lax.ppermute(piece, axes, pairs)
        full = lax.dynamic_update_slice_in_dim(full, piece, source * width, axis=2)
    return transform(full[0], full[1], dests)


def solution(mesh):
    placed = (
        P(None, ("uv", "rep"), None, None, None),
        P(("uv", "rep"), None, None),
        P(("uv", "rep"), None, None, None),
        P(("uv", "rep"), None, None, None),
        P(("uv", "rep"), None, None, None),
        P(),
    )
    return jax.shard_map(
        shards, mesh=mesh, in_specs=placed, out_specs=P(("uv", "rep"), None, None), check_vma=False
    )
```

```python
import functools
import math

import jax
import jax.numpy as jnp
from jax import lax
from jax.experimental import pallas as pl
from jax.experimental.pallas import tpu as pltpu
from jax.sharding import PartitionSpec as P

TILE = 128
SUPPORT = 8
GROUP = 16
FIELDS = 5


def make_table(first, second, length):
    index_a = lax.broadcasted_iota(jnp.int32, (first, second), 0)
    index_b = lax.broadcasted_iota(jnp.int32, (first, second), 1)
    angle = 2.0 * math.pi / length * (index_a * index_b % length).astype(jnp.float32)
    return (jnp.cos(angle), jnp.sin(angle))


def transform(field, groups):
    nrows = field.shape[1]
    total = field.shape[2]
    width = total // groups
    precision = lax.Precision.HIGH
    cos_a, sin_a = make_table(groups, groups, groups)
    cos_t, sin_t = make_table(groups, width, total)
    cos_b, sin_b = make_table(width, width, width)
    first_matrix = jnp.stack(
        [jnp.stack([cos_a, -sin_a], axis=1), jnp.stack([sin_a, cos_a], axis=1)]
    )
    scale = 1.0 / math.sqrt(total)
    final_matrix = jnp.stack(
        [jnp.stack([cos_b, -sin_b], axis=1), jnp.stack([sin_b, cos_b], axis=1)]
    ) * scale
    first = jnp.einsum(
        "crpj,cpdk->drkj", field.reshape(2, nrows, groups, width), first_matrix, precision=precision
    )
    turned = jnp.stack(
        [first[0] * cos_t + first[1] * sin_t, first[1] * cos_t - first[0] * sin_t]
    )
    final = jnp.einsum("drkj,djem->remk", turned, final_matrix, precision=precision)
    return final.reshape(nrows, 2, total)


def weigh(vis_re, vis_im, planes, kernels):
    nplanes = kernels.shape[0]
    width = kernels.shape[1]
    half = width // 2
    onehot = (
        planes[..., None] == lax.broadcasted_iota(jnp.int32, planes.shape + (nplanes,), planes.ndim)
    ).astype(jnp.float32)
    kern = jnp.dot(
        onehot.reshape(-1, nplanes),
        kernels,
        precision=lax.Precision.HIGHEST,
        preferred_element_type=jnp.float32,
    )
    kern = kern.reshape(planes.shape + (width,))
    kern_re = kern[..., :half]
    kern_im = kern[..., half:]
    part_re = vis_re[..., None] * kern_re - vis_im[..., None] * kern_im
    part_im = vis_re[..., None] * kern_im + vis_im[..., None] * kern_re
    return jnp.concatenate([part_re, part_im], axis=-1).astype(jnp.bfloat16)


def split3(values):
    high = lax.reduce_precision(values, exponent_bits=8, mantissa_bits=7)
    rest = values - high
    middle = lax.reduce_precision(rest, exponent_bits=8, mantissa_bits=7)
    low = rest - middle
    return high.astype(jnp.bfloat16), middle.astype(jnp.bfloat16), low.astype(jnp.bfloat16)


def grid_kernel(fld_ref, eye_ref, kt_ref, xv_ref, xu_ref, e_ref, out_ref, rep_ref, x_ref, r_ref, tab_ref):
    chunk_step = pl.program_id(1)
    chunk = fld_ref.shape[2]
    rows = out_ref.shape[1]
    ngroups = chunk // GROUP
    width = 2 * SUPPORT * SUPPORT
    nblocks = width // SUPPORT
    depth = nblocks * GROUP // 2
    nplanes = kt_ref.shape[0]

    @pl.when(chunk_step == 0)
    def _():
        out_ref[...] = jnp.zeros_like(out_ref)

    fld = fld_ref[0]
    cols = lax.dot_general(
        eye_ref[...], fld, (((1,), (1,)), ((), ())), preferred_element_type=jnp.float32
    )
    nf = fld.shape[0] // 3
    cols = (cols[:, 0:nf] + cols[:, nf:2 * nf]) + cols[:, 2 * nf:3 * nf]
    vis_re = cols[:, 0:1]
    vis_im = cols[:, 1:2]
    planes = cols[:, 2:3].astype(jnp.int32)
    onehot = (planes == lax.broadcasted_iota(jnp.int32, (chunk, nplanes), 1)).astype(jnp.bfloat16)
    parts = jnp.dot(onehot, kt_ref[...], preferred_element_type=jnp.float32)
    kern_a = (parts[:, 0:width] + parts[:, width:2 * width]) + parts[:, 2 * width:3 * width]
    kern_b = (parts[:, 3 * width:4 * width] + parts[:, 4 * width:5 * width]) + parts[:, 5 * width:6 * width]
    lane = lax.broadcasted_iota(jnp.int32, (chunk, width), 1)
    signed_im = jnp.where(lane < width // 2, -vis_im, vis_im)
    weighted = (vis_re * kern_a + signed_im * kern_b).astype(jnp.bfloat16)

    gmask = (
        lax.broadcasted_iota(jnp.int32, (ngroups, chunk), 1) // GROUP
        == lax.broadcasted_iota(jnp.int32, (ngroups, chunk), 0)
    )
    zero_row = jnp.zeros((ngroups, chunk), jnp.bfloat16)
    vo_rows = jnp.where(gmask, fld[4:5, :], zero_row)
    uo_rows = jnp.where(gmask, fld[3:4, :], zero_row)
    tlane = lax.broadcasted_iota(jnp.int32, (ngroups, TILE), 1)
    tab_ref[0] = jnp.dot(vo_rows, xv_ref[...], preferred_element_type=jnp.float32).astype(jnp.int32) + tlane % SUPPORT
    tab_ref[1] = jnp.dot(uo_rows, xu_ref[...], preferred_element_type=jnp.float32).astype(jnp.int32) + tlane // GROUP

    rep_ref[...] = jnp.dot(
        weighted, e_ref[...], preferred_element_type=jnp.float32
    ).astype(jnp.bfloat16)
    lane = lax.broadcasted_iota(jnp.int32, (GROUP, TILE), 1)
    row = lax.broadcasted_iota(jnp.int32, (GROUP, TILE), 0)
    keep = (lane // SUPPORT) == row
    vrow = lax.broadcasted_iota(jnp.int32, (TILE, TILE), 0)
    urow = lax.broadcasted_iota(jnp.int32, (rows, TILE), 0)
    zero = jnp.zeros((GROUP, TILE), jnp.bfloat16)

    def body(g, carry):
        start = pl.multiple_of(g * GROUP, GROUP)
        blocks = [
            jnp.where(keep, rep_ref[pl.ds(start, GROUP), pl.ds(i * TILE, TILE)], zero)
            for i in range(nblocks)
        ]
        wbd = jnp.concatenate(blocks, axis=0)
        vob = tab_ref[0, pl.ds(g, 1), :]
        cst = (vrow == vob).astype(jnp.bfloat16)
        spread = lax.dot_general(
            wbd, cst, (((1,), (1,)), ((), ())), preferred_element_type=jnp.float32
        ).astype(jnp.bfloat16)
        at = pl.multiple_of(g * depth, depth)
        x_ref[0, pl.ds(at, depth), :] = spread[:depth]
        x_ref[1, pl.ds(at, depth), :] = spread[depth:]
        uoa = tab_ref[1, pl.ds(g, 1), :]
        r_ref[:, pl.ds(at, TILE)] = (urow == uoa).astype(jnp.bfloat16)
        return carry

    lax.fori_loop(0, ngroups, body, 0, unroll=True)
    pick = r_ref[...]
    out_ref[0] += jnp.dot(pick, x_ref[0], preferred_element_type=jnp.float32)
    out_ref[1] += jnp.dot(pick, x_ref[1], preferred_element_type=jnp.float32)


def grid_rows(fld, kernels, rows):
    dests, nf, per_dest = fld.shape
    chunk = per_dest
    for size in (384, 192, 96, 48, 16):
        if per_dest % size == 0 and size <= per_dest:
            chunk = size
            break
    steps = per_dest // chunk
    ngroups = chunk // GROUP
    width = kernels.shape[1]
    half = width // 2
    nblocks = width // SUPPORT
    lanes_in = lax.broadcasted_iota(jnp.int32, (width, nblocks * TILE), 0)
    lanes_out = lax.broadcasted_iota(jnp.int32, (width, nblocks * TILE), 1)
    expand = (
        (lanes_in // SUPPORT == lanes_out // TILE) & (lanes_in % SUPPORT == lanes_out % SUPPORT)
    ).astype(jnp.bfloat16)
    eye = (
        lax.broadcasted_iota(jnp.int32, (chunk, chunk), 0)
        == lax.broadcasted_iota(jnp.int32, (chunk, chunk), 1)
    ).astype(jnp.bfloat16)
    swapped = jnp.concatenate([kernels[:, half:], kernels[:, :half]], axis=1)
    table = jnp.concatenate(split3(kernels) + split3(swapped), axis=1)
    n_in = lax.broadcasted_iota(jnp.int32, (chunk, TILE), 0) % GROUP
    lane_t = lax.broadcasted_iota(jnp.int32, (chunk, TILE), 1)
    expand_v = (n_in == lane_t // SUPPORT).astype(jnp.bfloat16)
    expand_u = (n_in == lane_t % GROUP).astype(jnp.bfloat16)
    whole = lambda d, c: (0, 0)
    return pl.pallas_call(
        grid_kernel,
        grid=(dests, steps),
        in_specs=[
            pl.BlockSpec((1, nf, chunk), lambda d, c: (d, 0, c)),
            pl.BlockSpec((chunk, chunk), whole),
            pl.BlockSpec(table.shape, whole),
            pl.BlockSpec((chunk, TILE), whole),
            pl.BlockSpec((chunk, TILE), whole),
            pl.BlockSpec((width, nblocks * TILE), whole),
        ],
        out_specs=pl.BlockSpec((2, rows, TILE), lambda d, c: (0, 0, d)),
        out_shape=jax.ShapeDtypeStruct((2, rows, dests * TILE), jnp.float32),
        scratch_shapes=[
            pltpu.VMEM((chunk, nblocks * TILE), jnp.bfloat16),
            pltpu.VMEM((2, chunk * SUPPORT, TILE), jnp.bfloat16),
            pltpu.VMEM((rows, chunk * SUPPORT), jnp.bfloat16),
            pltpu.VMEM((2, ngroups, TILE), jnp.int32),
        ],
        compiler_params=pltpu.CompilerParams(
            dimension_semantics=("arbitrary", "arbitrary")
        ),
    )(fld, eye, table, expand_v, expand_u, expand)


def shards(visibilities, tile_counts, w_plane, u_offset, v_offset, kernels):
    dests = visibilities.shape[2]
    ntiles = visibilities.shape[3]
    slots = visibilities.shape[4]
    axes = ("uv", "rep")
    ndev = lax.axis_size(axes)
    rows = ntiles * TILE // ndev
    per_tile = ndev // ntiles
    own_dests = dests // per_tile
    me = lax.axis_index(axes)
    member = me % per_tile
    live = (
        lax.broadcasted_iota(jnp.int32, (dests, ntiles, slots), 2) < tile_counts[0][:, :, None]
    ).astype(jnp.float32)
    fields = jnp.concatenate(
        [
            visibilities[0, 0] * live,
            visibilities[1, 0] * live,
            w_plane[0].astype(jnp.float32),
            u_offset[0].astype(jnp.float32),
            v_offset[0].astype(jnp.float32),
        ],
        axis=-1,
    )
    send = fields.reshape(per_tile, own_dests, ntiles, FIELDS * slots).transpose(2, 0, 1, 3)
    send = send.reshape(ndev, own_dests * FIELDS * slots)
    got = lax.all_to_all(send, axes, split_axis=0, concat_axis=0, tiled=True)
    got = got.reshape(ndev, own_dests, FIELDS, slots).transpose(1, 2, 0, 3)
    got = got.reshape(own_dests, FIELDS, ndev * slots)
    got = jnp.pad(got, ((0, 0), (0, 8 - FIELDS), (0, 0)))
    got = jnp.concatenate(split3(got), axis=1)
    slab = grid_rows(got, kernels, TILE)
    width = own_dests * TILE
    mine = lax.dynamic_slice_in_dim(slab, member * rows, rows, axis=1)
    full = jnp.zeros((2, rows, dests * TILE), jnp.float32)
    full = lax.dynamic_update_slice_in_dim(full, mine, member * width, axis=2)
    for step in range(1, per_tile):
        target = (member + step) % per_tile
        source = (member + per_tile - step) % per_tile
        pairs = [
            (k, (k // per_tile) * per_tile + (k % per_tile + step) % per_tile)
            for k in range(ndev)
        ]
        piece = lax.dynamic_slice_in_dim(slab, target * rows, rows, axis=1)
        piece = lax.ppermute(piece, axes, pairs)
        full = lax.dynamic_update_slice_in_dim(full, piece, source * width, axis=2)
    return transform(full, dests)


def solution(mesh):
    placed = (
        P(None, ("uv", "rep"), None, None, None),
        P(("uv", "rep"), None, None),
        P(("uv", "rep"), None, None, None),
        P(("uv", "rep"), None, None, None),
        P(("uv", "rep"), None, None, None),
        P(),
    )
    return jax.shard_map(
        shards, mesh=mesh, in_specs=placed, out_specs=P(("uv", "rep"), None, None), check_vma=False
    )
```

```python
import functools
import math

import jax
import jax.numpy as jnp
from jax import lax
from jax.experimental import pallas as pl
from jax.experimental.pallas import tpu as pltpu
from jax.sharding import PartitionSpec as P

TILE = 128
SUPPORT = 8
GROUP = 16
FIELDS = 6


def make_table(first, second, length):
    index_a = lax.broadcasted_iota(jnp.int32, (first, second), 0)
    index_b = lax.broadcasted_iota(jnp.int32, (first, second), 1)
    angle = 2.0 * math.pi / length * (index_a * index_b % length).astype(jnp.float32)
    return (jnp.cos(angle), jnp.sin(angle))


def transform(field, groups):
    nrows = field.shape[1]
    total = field.shape[2]
    width = total // groups
    precision = lax.Precision.HIGH
    cos_a, sin_a = make_table(groups, groups, groups)
    cos_t, sin_t = make_table(groups, width, total)
    cos_b, sin_b = make_table(width, width, width)
    first_matrix = jnp.stack(
        [jnp.stack([cos_a, -sin_a], axis=1), jnp.stack([sin_a, cos_a], axis=1)]
    )
    scale = 1.0 / math.sqrt(total)
    final_matrix = jnp.stack(
        [jnp.stack([cos_b, -sin_b], axis=1), jnp.stack([sin_b, cos_b], axis=1)]
    ) * scale
    first = jnp.einsum(
        "crpj,cpdk->drkj", field.reshape(2, nrows, groups, width), first_matrix, precision=precision
    )
    turned = jnp.stack(
        [first[0] * cos_t + first[1] * sin_t, first[1] * cos_t - first[0] * sin_t]
    )
    final = jnp.einsum("drkj,djem->remk", turned, final_matrix, precision=precision)
    return final.reshape(nrows, 2, total)


def weigh(vis_re, vis_im, planes, kernels):
    nplanes = kernels.shape[0]
    width = kernels.shape[1]
    half = width // 2
    onehot = (
        planes[..., None] == lax.broadcasted_iota(jnp.int32, planes.shape + (nplanes,), planes.ndim)
    ).astype(jnp.float32)
    kern = jnp.dot(
        onehot.reshape(-1, nplanes),
        kernels,
        precision=lax.Precision.HIGHEST,
        preferred_element_type=jnp.float32,
    )
    kern = kern.reshape(planes.shape + (width,))
    kern_re = kern[..., :half]
    kern_im = kern[..., half:]
    part_re = vis_re[..., None] * kern_re - vis_im[..., None] * kern_im
    part_im = vis_re[..., None] * kern_im + vis_im[..., None] * kern_re
    return jnp.concatenate([part_re, part_im], axis=-1).astype(jnp.bfloat16)


def split3(values):
    high = lax.reduce_precision(values, exponent_bits=8, mantissa_bits=7)
    rest = values - high
    middle = lax.reduce_precision(rest, exponent_bits=8, mantissa_bits=7)
    low = rest - middle
    return high.astype(jnp.bfloat16), middle.astype(jnp.bfloat16), low.astype(jnp.bfloat16)


def grid_kernel(flags_ref, fld_ref, eye_ref, kt_ref, xv_ref, xu_ref, e_ref, out_ref, rep_ref, x_ref, r_ref, tab_ref):
    chunk_step = pl.program_id(1)
    base = (pl.program_id(0) * pl.num_programs(1) + chunk_step) * (fld_ref.shape[2] // GROUP)
    chunk = fld_ref.shape[2]
    rows = out_ref.shape[1]
    ngroups = chunk // GROUP
    width = 2 * SUPPORT * SUPPORT
    nblocks = width // SUPPORT
    depth = nblocks * GROUP // 2
    nplanes = kt_ref.shape[0]

    @pl.when(chunk_step == 0)
    def _():
        out_ref[...] = jnp.zeros_like(out_ref)

    fld = fld_ref[0]
    cols = lax.dot_general(
        eye_ref[...], fld, (((1,), (1,)), ((), ())), preferred_element_type=jnp.float32
    )
    nf = fld.shape[0] // 3
    cols = (cols[:, 0:nf] + cols[:, nf:2 * nf]) + cols[:, 2 * nf:3 * nf]
    vis_re = cols[:, 0:1]
    vis_im = cols[:, 1:2]
    planes = cols[:, 2:3].astype(jnp.int32)
    onehot = (planes == lax.broadcasted_iota(jnp.int32, (chunk, nplanes), 1)).astype(jnp.bfloat16)
    parts = jnp.dot(onehot, kt_ref[...], preferred_element_type=jnp.float32)
    kern_a = (parts[:, 0:width] + parts[:, width:2 * width]) + parts[:, 2 * width:3 * width]
    kern_b = (parts[:, 3 * width:4 * width] + parts[:, 4 * width:5 * width]) + parts[:, 5 * width:6 * width]
    lane = lax.broadcasted_iota(jnp.int32, (chunk, width), 1)
    signed_im = jnp.where(lane < width // 2, -vis_im, vis_im)
    weighted = (vis_re * kern_a + signed_im * kern_b).astype(jnp.bfloat16)

    gmask = (
        lax.broadcasted_iota(jnp.int32, (ngroups, chunk), 1) // GROUP
        == lax.broadcasted_iota(jnp.int32, (ngroups, chunk), 0)
    )
    zero_row = jnp.zeros((ngroups, chunk), jnp.bfloat16)
    vo_rows = jnp.where(gmask, fld[4:5, :], zero_row)
    uo_rows = jnp.where(gmask, fld[3:4, :], zero_row)
    tlane = lax.broadcasted_iota(jnp.int32, (ngroups, TILE), 1)
    tab_ref[0] = jnp.dot(vo_rows, xv_ref[...], preferred_element_type=jnp.float32).astype(jnp.int32) + tlane % SUPPORT
    tab_ref[1] = jnp.dot(uo_rows, xu_ref[...], preferred_element_type=jnp.float32).astype(jnp.int32) + tlane // GROUP

    rep_ref[...] = jnp.dot(
        weighted, e_ref[...], preferred_element_type=jnp.float32
    ).astype(jnp.bfloat16)
    lane = lax.broadcasted_iota(jnp.int32, (GROUP, TILE), 1)
    row = lax.broadcasted_iota(jnp.int32, (GROUP, TILE), 0)
    keep = (lane // SUPPORT) == row
    vrow = lax.broadcasted_iota(jnp.int32, (TILE, TILE), 0)
    urow = lax.broadcasted_iota(jnp.int32, (rows, TILE), 0)
    zero = jnp.zeros((GROUP, TILE), jnp.bfloat16)

    def body(g):
        start = g * GROUP
        blocks = [
            jnp.where(keep, rep_ref[pl.ds(start, GROUP), pl.ds(i * TILE, TILE)], zero)
            for i in range(nblocks)
        ]
        wbd = jnp.concatenate(blocks, axis=0)
        vob = tab_ref[0, pl.ds(g, 1), :]
        cst = (vrow == vob).astype(jnp.bfloat16)
        spread = lax.dot_general(
            wbd, cst, (((1,), (1,)), ((), ())), preferred_element_type=jnp.float32
        ).astype(jnp.bfloat16)
        at = g * depth
        x_ref[0, pl.ds(at, depth), :] = spread[:depth]
        x_ref[1, pl.ds(at, depth), :] = spread[depth:]
        uoa = tab_ref[1, pl.ds(g, 1), :]
        r_ref[:, pl.ds(at, TILE)] = (urow == uoa).astype(jnp.bfloat16)

    def skip(g):
        at = g * depth
        x_ref[:, pl.ds(at, depth), :] = jnp.zeros((2, depth, TILE), jnp.bfloat16)
        r_ref[:, pl.ds(at, TILE)] = jnp.zeros((rows, TILE), jnp.bfloat16)

    for g in range(ngroups):
        flag = flags_ref[base + g]
        pl.when(flag > 0)(functools.partial(body, g))
        pl.when(flag == 0)(functools.partial(skip, g))
    pick = r_ref[...]
    out_ref[0] += jnp.dot(pick, x_ref[0], preferred_element_type=jnp.float32)
    out_ref[1] += jnp.dot(pick, x_ref[1], preferred_element_type=jnp.float32)


def grid_rows(flags, fld, kernels, rows):
    dests, nf, per_dest = fld.shape
    chunk = per_dest
    for size in (384, 192, 96, 48, 16):
        if per_dest % size == 0 and size <= per_dest:
            chunk = size
            break
    steps = per_dest // chunk
    ngroups = chunk // GROUP
    width = kernels.shape[1]
    half = width // 2
    nblocks = width // SUPPORT
    lanes_in = lax.broadcasted_iota(jnp.int32, (width, nblocks * TILE), 0)
    lanes_out = lax.broadcasted_iota(jnp.int32, (width, nblocks * TILE), 1)
    expand = (
        (lanes_in // SUPPORT == lanes_out // TILE) & (lanes_in % SUPPORT == lanes_out % SUPPORT)
    ).astype(jnp.bfloat16)
    eye = (
        lax.broadcasted_iota(jnp.int32, (chunk, chunk), 0)
        == lax.broadcasted_iota(jnp.int32, (chunk, chunk), 1)
    ).astype(jnp.bfloat16)
    swapped = jnp.concatenate([kernels[:, half:], kernels[:, :half]], axis=1)
    table = jnp.concatenate(split3(kernels) + split3(swapped), axis=1)
    n_in = lax.broadcasted_iota(jnp.int32, (chunk, TILE), 0) % GROUP
    lane_t = lax.broadcasted_iota(jnp.int32, (chunk, TILE), 1)
    expand_v = (n_in == lane_t // SUPPORT).astype(jnp.bfloat16)
    expand_u = (n_in == lane_t % GROUP).astype(jnp.bfloat16)
    whole = lambda d, c, flags: (0, 0)
    grid_spec = pltpu.PrefetchScalarGridSpec(
        num_scalar_prefetch=1,
        grid=(dests, steps),
        in_specs=[
            pl.BlockSpec((1, nf, chunk), lambda d, c, flags: (d, 0, c)),
            pl.BlockSpec((chunk, chunk), whole),
            pl.BlockSpec(table.shape, whole),
            pl.BlockSpec((chunk, TILE), whole),
            pl.BlockSpec((chunk, TILE), whole),
            pl.BlockSpec((width, nblocks * TILE), whole),
        ],
        out_specs=pl.BlockSpec((2, rows, TILE), lambda d, c, flags: (0, 0, d)),
        scratch_shapes=[
            pltpu.VMEM((chunk, nblocks * TILE), jnp.bfloat16),
            pltpu.VMEM((2, chunk * SUPPORT, TILE), jnp.bfloat16),
            pltpu.VMEM((rows, chunk * SUPPORT), jnp.bfloat16),
            pltpu.VMEM((2, ngroups, TILE), jnp.int32),
        ],
    )
    return pl.pallas_call(
        grid_kernel,
        grid_spec=grid_spec,
        out_shape=jax.ShapeDtypeStruct((2, rows, dests * TILE), jnp.float32),
        compiler_params=pltpu.CompilerParams(
            dimension_semantics=("arbitrary", "arbitrary")
        ),
    )(flags, fld, eye, table, expand_v, expand_u, expand)


def shards(visibilities, tile_counts, w_plane, u_offset, v_offset, kernels):
    dests = visibilities.shape[2]
    ntiles = visibilities.shape[3]
    slots = visibilities.shape[4]
    axes = ("uv", "rep")
    ndev = lax.axis_size(axes)
    rows = ntiles * TILE // ndev
    per_tile = ndev // ntiles
    own_dests = dests // per_tile
    me = lax.axis_index(axes)
    member = me % per_tile
    live = (
        lax.broadcasted_iota(jnp.int32, (dests, ntiles, slots), 2) < tile_counts[0][:, :, None]
    ).astype(jnp.float32)
    fields = jnp.concatenate(
        [
            visibilities[0, 0] * live,
            visibilities[1, 0] * live,
            w_plane[0].astype(jnp.float32),
            u_offset[0].astype(jnp.float32),
            v_offset[0].astype(jnp.float32),
            live,
        ],
        axis=-1,
    )
    send = fields.reshape(per_tile, own_dests, ntiles, FIELDS * slots).transpose(2, 0, 1, 3)
    send = send.reshape(ndev, own_dests * FIELDS * slots)
    got = lax.all_to_all(send, axes, split_axis=0, concat_axis=0, tiled=True)
    got = got.reshape(ndev, own_dests, FIELDS, slots).transpose(1, 2, 3, 0)
    got = got.reshape(own_dests, FIELDS, ndev * slots)
    flags = jnp.max(got[:, FIELDS - 1].reshape(own_dests, -1, GROUP), axis=2) > 0
    flags = flags.astype(jnp.int32).reshape(-1)
    got = jnp.pad(got, ((0, 0), (0, 8 - FIELDS), (0, 0)))
    got = jnp.concatenate(split3(got), axis=1)
    slab = grid_rows(flags, got, kernels, TILE)
    width = own_dests * TILE
    mine = lax.dynamic_slice_in_dim(slab, member * rows, rows, axis=1)
    full = jnp.zeros((2, rows, dests * TILE), jnp.float32)
    full = lax.dynamic_update_slice_in_dim(full, mine, member * width, axis=2)
    for step in range(1, per_tile):
        target = (member + step) % per_tile
        source = (member + per_tile - step) % per_tile
        pairs = [
            (k, (k // per_tile) * per_tile + (k % per_tile + step) % per_tile)
            for k in range(ndev)
        ]
        piece = lax.dynamic_slice_in_dim(slab, target * rows, rows, axis=1)
        piece = lax.ppermute(piece, axes, pairs)
        full = lax.dynamic_update_slice_in_dim(full, piece, source * width, axis=2)
    return transform(full, dests)


def solution(mesh):
    placed = (
        P(None, ("uv", "rep"), None, None, None),
        P(("uv", "rep"), None, None),
        P(("uv", "rep"), None, None, None),
        P(("uv", "rep"), None, None, None),
        P(("uv", "rep"), None, None, None),
        P(),
    )
    return jax.shard_map(
        shards, mesh=mesh, in_specs=placed, out_specs=P(("uv", "rep"), None, None), check_vma=False
    )
```

```python
import functools
import math

import jax
import jax.numpy as jnp
from jax import lax
from jax.experimental import pallas as pl
from jax.experimental.pallas import tpu as pltpu
from jax.sharding import PartitionSpec as P

TILE = 128
SUPPORT = 8
GROUP = 16
FIELDS = 5


def make_table(first, second, length):
    index_a = lax.broadcasted_iota(jnp.int32, (first, second), 0)
    index_b = lax.broadcasted_iota(jnp.int32, (first, second), 1)
    angle = 2.0 * math.pi / length * (index_a * index_b % length).astype(jnp.float32)
    return (jnp.cos(angle), jnp.sin(angle))


def transform(field, groups):
    nrows = field.shape[1]
    total = field.shape[2]
    width = total // groups
    precision = lax.Precision.HIGH
    cos_a, sin_a = make_table(groups, groups, groups)
    cos_t, sin_t = make_table(groups, width, total)
    cos_b, sin_b = make_table(width, width, width)
    first_matrix = jnp.stack(
        [jnp.stack([cos_a, -sin_a], axis=1), jnp.stack([sin_a, cos_a], axis=1)]
    )
    scale = 1.0 / math.sqrt(total)
    final_matrix = jnp.stack(
        [jnp.stack([cos_b, -sin_b], axis=1), jnp.stack([sin_b, cos_b], axis=1)]
    ) * scale
    first = jnp.einsum(
        "crpj,cpdk->drkj", field.reshape(2, nrows, groups, width), first_matrix, precision=precision
    )
    turned = jnp.stack(
        [first[0] * cos_t + first[1] * sin_t, first[1] * cos_t - first[0] * sin_t]
    )
    final = jnp.einsum("drkj,djem->remk", turned, final_matrix, precision=precision)
    return final.reshape(nrows, 2, total)


def weigh(vis_re, vis_im, planes, kernels):
    nplanes = kernels.shape[0]
    width = kernels.shape[1]
    half = width // 2
    onehot = (
        planes[..., None] == lax.broadcasted_iota(jnp.int32, planes.shape + (nplanes,), planes.ndim)
    ).astype(jnp.float32)
    kern = jnp.dot(
        onehot.reshape(-1, nplanes),
        kernels,
        precision=lax.Precision.HIGHEST,
        preferred_element_type=jnp.float32,
    )
    kern = kern.reshape(planes.shape + (width,))
    kern_re = kern[..., :half]
    kern_im = kern[..., half:]
    part_re = vis_re[..., None] * kern_re - vis_im[..., None] * kern_im
    part_im = vis_re[..., None] * kern_im + vis_im[..., None] * kern_re
    return jnp.concatenate([part_re, part_im], axis=-1).astype(jnp.bfloat16)


def split3(values):
    high = lax.reduce_precision(values, exponent_bits=8, mantissa_bits=7)
    rest = values - high
    middle = lax.reduce_precision(rest, exponent_bits=8, mantissa_bits=7)
    low = rest - middle
    return high.astype(jnp.bfloat16), middle.astype(jnp.bfloat16), low.astype(jnp.bfloat16)


def grid_kernel(fld_ref, eye_ref, kt_ref, xv_ref, xu_ref, e_ref, out_ref, rep_ref, x_ref, r_ref, tab_ref):
    chunk_step = pl.program_id(1)
    chunk = fld_ref.shape[2]
    rows = out_ref.shape[1]
    ngroups = chunk // GROUP
    width = 2 * SUPPORT * SUPPORT
    nblocks = width // SUPPORT
    depth = nblocks * GROUP // 2
    nplanes = kt_ref.shape[0]

    @pl.when(chunk_step == 0)
    def _():
        out_ref[...] = jnp.zeros_like(out_ref)

    fld = fld_ref[0]
    cols = lax.dot_general(
        eye_ref[...], fld, (((1,), (1,)), ((), ())), preferred_element_type=jnp.float32
    )
    nf = fld.shape[0] // 3
    cols = (cols[:, 0:nf] + cols[:, nf:2 * nf]) + cols[:, 2 * nf:3 * nf]
    vis_re = cols[:, 0:1]
    vis_im = cols[:, 1:2]
    planes = cols[:, 2:3].astype(jnp.int32)
    onehot = (planes == lax.broadcasted_iota(jnp.int32, (chunk, nplanes), 1)).astype(jnp.bfloat16)
    parts = jnp.dot(onehot, kt_ref[...], preferred_element_type=jnp.float32)
    kern_a = (parts[:, 0:width] + parts[:, width:2 * width]) + parts[:, 2 * width:3 * width]
    kern_b = (parts[:, 3 * width:4 * width] + parts[:, 4 * width:5 * width]) + parts[:, 5 * width:6 * width]
    lane = lax.broadcasted_iota(jnp.int32, (chunk, width), 1)
    signed_im = jnp.where(lane < width // 2, -vis_im, vis_im)
    weighted = (vis_re * kern_a + signed_im * kern_b).astype(jnp.bfloat16)

    gmask = (
        lax.broadcasted_iota(jnp.int32, (ngroups, chunk), 1) // GROUP
        == lax.broadcasted_iota(jnp.int32, (ngroups, chunk), 0)
    )
    zero_row = jnp.zeros((ngroups, chunk), jnp.bfloat16)
    vo_rows = jnp.where(gmask, fld[4:5, :], zero_row)
    uo_rows = jnp.where(gmask, fld[3:4, :], zero_row)
    tlane = lax.broadcasted_iota(jnp.int32, (ngroups, TILE), 1)
    tab_ref[0] = jnp.dot(vo_rows, xv_ref[...], preferred_element_type=jnp.float32).astype(jnp.int32) + tlane % SUPPORT
    tab_ref[1] = jnp.dot(uo_rows, xu_ref[...], preferred_element_type=jnp.float32).astype(jnp.int32) + tlane // GROUP

    rep_ref[...] = weighted.astype(jnp.float32)
    lane = lax.broadcasted_iota(jnp.int32, (GROUP, TILE), 1)
    row = lax.broadcasted_iota(jnp.int32, (GROUP, TILE), 0)
    keep = (lane // SUPPORT) == row
    vrow = lax.broadcasted_iota(jnp.int32, (TILE, TILE), 0)
    urow = lax.broadcasted_iota(jnp.int32, (rows, TILE), 0)
    zero = jnp.zeros((GROUP, TILE), jnp.float32)

    def body(g, carry):
        start = pl.multiple_of(g * GROUP, GROUP)
        halves = [rep_ref[pl.ds(start + h * 8, 8), :] for h in range(GROUP // 8)]
        pre = [pltpu.roll(v, TILE // 2, 1) for v in halves]
        blocks = []
        for i in range(nblocks):
            for h in range(GROUP // 8):
                shift = (h * 8 * SUPPORT - i * SUPPORT) % TILE
                if shift + 7 * SUPPORT < TILE:
                    moved = pltpu.roll(halves[h], shift, 1, stride=SUPPORT, stride_axis=0)
                else:
                    moved = pltpu.roll(pre[h], shift - TILE // 2, 1, stride=SUPPORT, stride_axis=0)
                blocks.append(jnp.where(keep[h * 8:(h + 1) * 8], moved, zero[:8]))
        wbd = jnp.concatenate(blocks, axis=0).astype(jnp.bfloat16)
        vob = tab_ref[0, pl.ds(g, 1), :]
        cst = (vrow == vob).astype(jnp.bfloat16)
        spread = lax.dot_general(
            wbd, cst, (((1,), (1,)), ((), ())), preferred_element_type=jnp.float32
        ).astype(jnp.bfloat16)
        at = pl.multiple_of(g * depth, depth)
        x_ref[0, pl.ds(at, depth), :] = spread[:depth]
        x_ref[1, pl.ds(at, depth), :] = spread[depth:]
        uoa = tab_ref[1, pl.ds(g, 1), :]
        r_ref[:, pl.ds(at, TILE)] = (urow == uoa).astype(jnp.bfloat16)
        return carry

    lax.fori_loop(0, ngroups, body, 0, unroll=True)
    pick = r_ref[...]
    out_ref[0] += jnp.dot(pick, x_ref[0], preferred_element_type=jnp.float32)
    out_ref[1] += jnp.dot(pick, x_ref[1], preferred_element_type=jnp.float32)


def grid_rows(fld, kernels, rows):
    dests, nf, per_dest = fld.shape
    chunk = per_dest
    for size in (384, 192, 96, 48, 16):
        if per_dest % size == 0 and size <= per_dest:
            chunk = size
            break
    steps = per_dest // chunk
    ngroups = chunk // GROUP
    width = kernels.shape[1]
    half = width // 2
    nblocks = width // SUPPORT
    lanes_in = lax.broadcasted_iota(jnp.int32, (width, nblocks * TILE), 0)
    lanes_out = lax.broadcasted_iota(jnp.int32, (width, nblocks * TILE), 1)
    expand = (
        (lanes_in // SUPPORT == lanes_out // TILE) & (lanes_in % SUPPORT == lanes_out % SUPPORT)
    ).astype(jnp.bfloat16)
    eye = (
        lax.broadcasted_iota(jnp.int32, (chunk, chunk), 0)
        == lax.broadcasted_iota(jnp.int32, (chunk, chunk), 1)
    ).astype(jnp.bfloat16)
    swapped = jnp.concatenate([kernels[:, half:], kernels[:, :half]], axis=1)
    table = jnp.concatenate(split3(kernels) + split3(swapped), axis=1)
    n_in = lax.broadcasted_iota(jnp.int32, (chunk, TILE), 0) % GROUP
    lane_t = lax.broadcasted_iota(jnp.int32, (chunk, TILE), 1)
    expand_v = (n_in == lane_t // SUPPORT).astype(jnp.bfloat16)
    expand_u = (n_in == lane_t % GROUP).astype(jnp.bfloat16)
    whole = lambda d, c: (0, 0)
    return pl.pallas_call(
        grid_kernel,
        grid=(dests, steps),
        in_specs=[
            pl.BlockSpec((1, nf, chunk), lambda d, c: (d, 0, c)),
            pl.BlockSpec((chunk, chunk), whole),
            pl.BlockSpec(table.shape, whole),
            pl.BlockSpec((chunk, TILE), whole),
            pl.BlockSpec((chunk, TILE), whole),
            pl.BlockSpec((width, nblocks * TILE), whole),
        ],
        out_specs=pl.BlockSpec((2, rows, TILE), lambda d, c: (0, 0, d)),
        out_shape=jax.ShapeDtypeStruct((2, rows, dests * TILE), jnp.float32),
        scratch_shapes=[
            pltpu.VMEM((chunk, width), jnp.float32),
            pltpu.VMEM((2, chunk * SUPPORT, TILE), jnp.bfloat16),
            pltpu.VMEM((rows, chunk * SUPPORT), jnp.bfloat16),
            pltpu.VMEM((2, ngroups, TILE), jnp.int32),
        ],
        compiler_params=pltpu.CompilerParams(
            dimension_semantics=("arbitrary", "arbitrary")
        ),
    )(fld, eye, table, expand_v, expand_u, expand)


def shards(visibilities, tile_counts, w_plane, u_offset, v_offset, kernels):
    dests = visibilities.shape[2]
    ntiles = visibilities.shape[3]
    slots = visibilities.shape[4]
    axes = ("uv", "rep")
    ndev = lax.axis_size(axes)
    rows = ntiles * TILE // ndev
    per_tile = ndev // ntiles
    own_dests = dests // per_tile
    me = lax.axis_index(axes)
    member = me % per_tile
    live = (
        lax.broadcasted_iota(jnp.int32, (dests, ntiles, slots), 2) < tile_counts[0][:, :, None]
    ).astype(jnp.float32)
    fields = jnp.concatenate(
        [
            visibilities[0, 0] * live,
            visibilities[1, 0] * live,
            w_plane[0].astype(jnp.float32),
            u_offset[0].astype(jnp.float32),
            v_offset[0].astype(jnp.float32),
        ],
        axis=-1,
    )
    send = fields.reshape(per_tile, own_dests, ntiles, FIELDS * slots).transpose(2, 0, 1, 3)
    send = send.reshape(ndev, own_dests * FIELDS * slots)
    got = lax.all_to_all(send, axes, split_axis=0, concat_axis=0, tiled=True)
    got = got.reshape(ndev, own_dests, FIELDS, slots).transpose(1, 2, 0, 3)
    got = got.reshape(own_dests, FIELDS, ndev * slots)
    got = jnp.pad(got, ((0, 0), (0, 8 - FIELDS), (0, 0)))
    got = jnp.concatenate(split3(got), axis=1)
    slab = grid_rows(got, kernels, TILE)
    width = own_dests * TILE
    mine = lax.dynamic_slice_in_dim(slab, member * rows, rows, axis=1)
    full = jnp.zeros((2, rows, dests * TILE), jnp.float32)
    full = lax.dynamic_update_slice_in_dim(full, mine, member * width, axis=2)
    for step in range(1, per_tile):
        target = (member + step) % per_tile
        source = (member + per_tile - step) % per_tile
        pairs = [
            (k, (k // per_tile) * per_tile + (k % per_tile + step) % per_tile)
            for k in range(ndev)
        ]
        piece = lax.dynamic_slice_in_dim(slab, target * rows, rows, axis=1)
        piece = lax.ppermute(piece, axes, pairs)
        full = lax.dynamic_update_slice_in_dim(full, piece, source * width, axis=2)
    return transform(full, dests)


def solution(mesh):
    placed = (
        P(None, ("uv", "rep"), None, None, None),
        P(("uv", "rep"), None, None),
        P(("uv", "rep"), None, None, None),
        P(("uv", "rep"), None, None, None),
        P(("uv", "rep"), None, None, None),
        P(),
    )
    return jax.shard_map(
        shards, mesh=mesh, in_specs=placed, out_specs=P(("uv", "rep"), None, None), check_vma=False
    )
```

```python
import functools
import math

import jax
import jax.numpy as jnp
from jax import lax
from jax.experimental import pallas as pl
from jax.experimental.pallas import tpu as pltpu
from jax.sharding import PartitionSpec as P

TILE = 128
SUPPORT = 8
GROUP = 16
FIELDS = 5


def make_table(first, second, length):
    index_a = lax.broadcasted_iota(jnp.int32, (first, second), 0)
    index_b = lax.broadcasted_iota(jnp.int32, (first, second), 1)
    angle = 2.0 * math.pi / length * (index_a * index_b % length).astype(jnp.float32)
    return (jnp.cos(angle), jnp.sin(angle))


def transform(field, groups):
    nrows = field.shape[1]
    total = field.shape[2]
    width = total // groups
    precision = lax.Precision.HIGH
    cos_a, sin_a = make_table(groups, groups, groups)
    cos_t, sin_t = make_table(groups, width, total)
    cos_b, sin_b = make_table(width, width, width)
    first_matrix = jnp.stack(
        [jnp.stack([cos_a, -sin_a], axis=1), jnp.stack([sin_a, cos_a], axis=1)]
    )
    scale = 1.0 / math.sqrt(total)
    final_matrix = jnp.stack(
        [jnp.stack([cos_b, -sin_b], axis=1), jnp.stack([sin_b, cos_b], axis=1)]
    ) * scale
    first = jnp.einsum(
        "crpj,cpdk->drkj", field.reshape(2, nrows, groups, width), first_matrix, precision=precision
    )
    turned = jnp.stack(
        [first[0] * cos_t + first[1] * sin_t, first[1] * cos_t - first[0] * sin_t]
    )
    final = jnp.einsum("drkj,djem->remk", turned, final_matrix, precision=precision)
    return final.reshape(nrows, 2, total)


def split3(values):
    high = lax.reduce_precision(values, exponent_bits=8, mantissa_bits=7)
    rest = values - high
    middle = lax.reduce_precision(rest, exponent_bits=8, mantissa_bits=7)
    low = rest - middle
    return high.astype(jnp.bfloat16), middle.astype(jnp.bfloat16), low.astype(jnp.bfloat16)


def grid_kernel(fld_ref, eye_ref, kt_ref, xv_ref, xu_ref, out_ref, rep_ref, x_ref, r_ref, tab_ref):
    chunk_step = pl.program_id(1)
    chunk = fld_ref.shape[2]
    rows = out_ref.shape[1]
    ngroups = chunk // GROUP
    width = 2 * SUPPORT * SUPPORT
    nblocks = width // SUPPORT
    depth = nblocks * GROUP // 2
    nplanes = kt_ref.shape[0]

    @pl.when(chunk_step == 0)
    def _():
        out_ref[...] = jnp.zeros_like(out_ref)

    fld = fld_ref[0]
    cols = lax.dot_general(
        eye_ref[...], fld, (((1,), (1,)), ((), ())), preferred_element_type=jnp.float32
    )
    nf = fld.shape[0] // 3
    cols = (cols[:, 0:nf] + cols[:, nf:2 * nf]) + cols[:, 2 * nf:3 * nf]
    vis_re = cols[:, 0:1]
    vis_im = cols[:, 1:2]
    planes = cols[:, 2:3].astype(jnp.int32)
    onehot = (planes == lax.broadcasted_iota(jnp.int32, (chunk, nplanes), 1)).astype(jnp.bfloat16)
    parts = jnp.dot(onehot, kt_ref[...], preferred_element_type=jnp.float32)
    kern_a = (parts[:, 0:width] + parts[:, width:2 * width]) + parts[:, 2 * width:3 * width]
    kern_b = pltpu.roll(kern_a, width // 2, 1)
    lane = lax.broadcasted_iota(jnp.int32, (chunk, width), 1)
    signed_im = jnp.where(lane < width // 2, -vis_im, vis_im)
    weighted = (vis_re * kern_a + signed_im * kern_b).astype(jnp.bfloat16)

    gmask = (
        lax.broadcasted_iota(jnp.int32, (ngroups, chunk), 1) // GROUP
        == lax.broadcasted_iota(jnp.int32, (ngroups, chunk), 0)
    )
    zero_row = jnp.zeros((ngroups, chunk), jnp.bfloat16)
    vo_rows = jnp.where(gmask, fld[4:5, :], zero_row)
    uo_rows = jnp.where(gmask, fld[3:4, :], zero_row)
    tlane = lax.broadcasted_iota(jnp.int32, (ngroups, TILE), 1)
    tab_ref[0] = jnp.dot(vo_rows, xv_ref[...], preferred_element_type=jnp.float32).astype(jnp.int32) + tlane % SUPPORT
    tab_ref[1] = jnp.dot(uo_rows, xu_ref[...], preferred_element_type=jnp.float32).astype(jnp.int32) + tlane // GROUP

    rep_ref[...] = weighted.astype(jnp.float32)
    lane = lax.broadcasted_iota(jnp.int32, (GROUP, TILE), 1)
    row = lax.broadcasted_iota(jnp.int32, (GROUP, TILE), 0)
    keep = (lane // SUPPORT) == row
    vrow = lax.broadcasted_iota(jnp.int32, (TILE, TILE), 0)
    urow = lax.broadcasted_iota(jnp.int32, (rows, TILE), 0)
    zero = jnp.zeros((GROUP, TILE), jnp.float32)

    def body(g, carry):
        start = pl.multiple_of(g * GROUP, GROUP)
        halves = [rep_ref[pl.ds(start + h * 8, 8), :] for h in range(GROUP // 8)]
        pre = [pltpu.roll(v, TILE // 2, 1) for v in halves]
        blocks = []
        for i in range(nblocks):
            for h in range(GROUP // 8):
                shift = (h * 8 * SUPPORT - i * SUPPORT) % TILE
                if shift + 7 * SUPPORT < TILE:
                    moved = pltpu.roll(halves[h], shift, 1, stride=SUPPORT, stride_axis=0)
                else:
                    moved = pltpu.roll(pre[h], shift - TILE // 2, 1, stride=SUPPORT, stride_axis=0)
                blocks.append(jnp.where(keep[h * 8:(h + 1) * 8], moved, zero[:8]))
        wbd = jnp.concatenate(blocks, axis=0).astype(jnp.bfloat16)
        vob = tab_ref[0, pl.ds(g, 1), :]
        cst = (vrow == vob).astype(jnp.bfloat16)
        spread = lax.dot_general(
            wbd, cst, (((1,), (1,)), ((), ())), preferred_element_type=jnp.float32
        ).astype(jnp.bfloat16)
        at = pl.multiple_of(g * depth, depth)
        x_ref[0, pl.ds(at, depth), :] = spread[:depth]
        x_ref[1, pl.ds(at, depth), :] = spread[depth:]
        uoa = tab_ref[1, pl.ds(g, 1), :]
        r_ref[:, pl.ds(at, TILE)] = (urow == uoa).astype(jnp.bfloat16)
        return carry

    lax.fori_loop(0, ngroups, body, 0, unroll=True)
    pick = r_ref[...]
    out_ref[0] += jnp.dot(pick, x_ref[0], preferred_element_type=jnp.float32)
    out_ref[1] += jnp.dot(pick, x_ref[1], preferred_element_type=jnp.float32)


def grid_rows(fld, kernels, rows):
    dests, nf, per_dest = fld.shape
    chunk = per_dest
    for size in (384, 192, 96, 48, 16):
        if per_dest % size == 0 and size <= per_dest:
            chunk = size
            break
    steps = per_dest // chunk
    ngroups = chunk // GROUP
    width = kernels.shape[1]
    half = width // 2
    nblocks = width // SUPPORT
    eye = (
        lax.broadcasted_iota(jnp.int32, (chunk, chunk), 0)
        == lax.broadcasted_iota(jnp.int32, (chunk, chunk), 1)
    ).astype(jnp.bfloat16)
    table = jnp.concatenate(split3(kernels), axis=1)
    n_in = lax.broadcasted_iota(jnp.int32, (chunk, TILE), 0) % GROUP
    lane_t = lax.broadcasted_iota(jnp.int32, (chunk, TILE), 1)
    expand_v = (n_in == lane_t // SUPPORT).astype(jnp.bfloat16)
    expand_u = (n_in == lane_t % GROUP).astype(jnp.bfloat16)
    whole = lambda d, c: (0, 0)
    return pl.pallas_call(
        grid_kernel,
        grid=(dests, steps),
        in_specs=[
            pl.BlockSpec((1, nf, chunk), lambda d, c: (d, 0, c)),
            pl.BlockSpec((chunk, chunk), whole),
            pl.BlockSpec(table.shape, whole),
            pl.BlockSpec((chunk, TILE), whole),
            pl.BlockSpec((chunk, TILE), whole),
        ],
        out_specs=pl.BlockSpec((2, rows, TILE), lambda d, c: (0, 0, d)),
        out_shape=jax.ShapeDtypeStruct((2, rows, dests * TILE), jnp.float32),
        scratch_shapes=[
            pltpu.VMEM((chunk, width), jnp.float32),
            pltpu.VMEM((2, chunk * SUPPORT, TILE), jnp.bfloat16),
            pltpu.VMEM((rows, chunk * SUPPORT), jnp.bfloat16),
            pltpu.VMEM((2, ngroups, TILE), jnp.int32),
        ],
        compiler_params=pltpu.CompilerParams(
            dimension_semantics=("arbitrary", "arbitrary")
        ),
    )(fld, eye, table, expand_v, expand_u)


def shards(visibilities, tile_counts, w_plane, u_offset, v_offset, kernels):
    dests = visibilities.shape[2]
    ntiles = visibilities.shape[3]
    slots = visibilities.shape[4]
    axes = ("uv", "rep")
    ndev = lax.axis_size(axes)
    rows = ntiles * TILE // ndev
    per_tile = ndev // ntiles
    own_dests = dests // per_tile
    me = lax.axis_index(axes)
    member = me % per_tile
    live = (
        lax.broadcasted_iota(jnp.int32, (dests, ntiles, slots), 2) < tile_counts[0][:, :, None]
    ).astype(jnp.float32)
    fields = jnp.concatenate(
        [
            visibilities[0, 0] * live,
            visibilities[1, 0] * live,
            w_plane[0].astype(jnp.float32),
            u_offset[0].astype(jnp.float32),
            v_offset[0].astype(jnp.float32),
        ],
        axis=-1,
    )
    send = fields.reshape(per_tile, own_dests, ntiles, FIELDS * slots).transpose(2, 0, 1, 3)
    send = send.reshape(ndev, own_dests * FIELDS * slots)
    got = lax.all_to_all(send, axes, split_axis=0, concat_axis=0, tiled=True)
    got = got.reshape(ndev, own_dests, FIELDS, slots).transpose(1, 2, 0, 3)
    got = got.reshape(own_dests, FIELDS, ndev * slots)
    got = jnp.pad(got, ((0, 0), (0, 8 - FIELDS), (0, 0)))
    got = jnp.concatenate(split3(got), axis=1)
    slab = grid_rows(got, kernels, TILE)
    width = own_dests * TILE
    mine = lax.dynamic_slice_in_dim(slab, member * rows, rows, axis=1)
    full = jnp.zeros((2, rows, dests * TILE), jnp.float32)
    full = lax.dynamic_update_slice_in_dim(full, mine, member * width, axis=2)
    for step in range(1, per_tile):
        target = (member + step) % per_tile
        source = (member + per_tile - step) % per_tile
        pairs = [
            (k, (k // per_tile) * per_tile + (k % per_tile + step) % per_tile)
            for k in range(ndev)
        ]
        piece = lax.dynamic_slice_in_dim(slab, target * rows, rows, axis=1)
        piece = lax.ppermute(piece, axes, pairs)
        full = lax.dynamic_update_slice_in_dim(full, piece, source * width, axis=2)
    return transform(full, dests)


def solution(mesh):
    placed = (
        P(None, ("uv", "rep"), None, None, None),
        P(("uv", "rep"), None, None),
        P(("uv", "rep"), None, None, None),
        P(("uv", "rep"), None, None, None),
        P(("uv", "rep"), None, None, None),
        P(),
    )
    return jax.shard_map(
        shards, mesh=mesh, in_specs=placed, out_specs=P(("uv", "rep"), None, None), check_vma=False
    )
```

```python
import functools
import math

import jax
import jax.numpy as jnp
from jax import lax
from jax.experimental import pallas as pl
from jax.experimental.pallas import tpu as pltpu
from jax.sharding import PartitionSpec as P

TILE = 128
SUPPORT = 8
GROUP = 16
FIELDS = 5


def make_table(first, second, length):
    index_a = lax.broadcasted_iota(jnp.int32, (first, second), 0)
    index_b = lax.broadcasted_iota(jnp.int32, (first, second), 1)
    angle = 2.0 * math.pi / length * (index_a * index_b % length).astype(jnp.float32)
    return (jnp.cos(angle), jnp.sin(angle))


def transform(field, groups):
    nrows = field.shape[1]
    total = field.shape[2]
    width = total // groups
    precision = lax.Precision.HIGH
    cos_a, sin_a = make_table(groups, groups, groups)
    cos_t, sin_t = make_table(groups, width, total)
    cos_b, sin_b = make_table(width, width, width)
    first_matrix = jnp.stack(
        [jnp.stack([cos_a, -sin_a], axis=1), jnp.stack([sin_a, cos_a], axis=1)]
    )
    scale = 1.0 / math.sqrt(total)
    final_matrix = jnp.stack(
        [jnp.stack([cos_b, -sin_b], axis=1), jnp.stack([sin_b, cos_b], axis=1)]
    ) * scale
    first = jnp.einsum(
        "crpj,cpdk->drkj", field.reshape(2, nrows, groups, width), first_matrix, precision=precision
    )
    turned = jnp.stack(
        [first[0] * cos_t + first[1] * sin_t, first[1] * cos_t - first[0] * sin_t]
    )
    final = jnp.einsum("drkj,djem->remk", turned, final_matrix, precision=precision)
    return final.reshape(nrows, 2, total)


def split3(values):
    high = lax.reduce_precision(values, exponent_bits=8, mantissa_bits=7)
    rest = values - high
    middle = lax.reduce_precision(rest, exponent_bits=8, mantissa_bits=7)
    low = rest - middle
    return high.astype(jnp.bfloat16), middle.astype(jnp.bfloat16), low.astype(jnp.bfloat16)


def grid_kernel(*refs):
    if len(refs) == 11:
        member_ref, fld_ref, eye_ref, kt_ref, xv_ref, xu_ref, out_ref, other_ref, rep_ref, x_ref, r_ref, tab_ref = (None,) + refs
    else:
        member_ref, fld_ref, eye_ref, kt_ref, xv_ref, xu_ref, out_ref, other_ref, rep_ref, x_ref, r_ref, tab_ref = refs
    chunk_step = pl.program_id(1)
    chunk = fld_ref.shape[2]
    rows = r_ref.shape[0]
    ngroups = chunk // GROUP
    width = 2 * SUPPORT * SUPPORT
    nblocks = width // SUPPORT
    depth = nblocks * GROUP // 2
    nplanes = kt_ref.shape[0]

    @pl.when(chunk_step == 0)
    def _():
        out_ref[...] = jnp.zeros_like(out_ref)
        other_ref[...] = jnp.zeros_like(other_ref)

    fld = fld_ref[0]
    cols = lax.dot_general(
        eye_ref[...], fld, (((1,), (1,)), ((), ())), preferred_element_type=jnp.float32
    )
    nf = fld.shape[0] // 3
    cols = (cols[:, 0:nf] + cols[:, nf:2 * nf]) + cols[:, 2 * nf:3 * nf]
    vis_re = cols[:, 0:1]
    vis_im = cols[:, 1:2]
    planes = cols[:, 2:3].astype(jnp.int32)
    onehot = (planes == lax.broadcasted_iota(jnp.int32, (chunk, nplanes), 1)).astype(jnp.bfloat16)
    parts = jnp.dot(onehot, kt_ref[...], preferred_element_type=jnp.float32)
    kern_a = (parts[:, 0:width] + parts[:, width:2 * width]) + parts[:, 2 * width:3 * width]
    kern_b = pltpu.roll(kern_a, width // 2, 1)
    lane = lax.broadcasted_iota(jnp.int32, (chunk, width), 1)
    signed_im = jnp.where(lane < width // 2, -vis_im, vis_im)
    weighted = (vis_re * kern_a + signed_im * kern_b).astype(jnp.bfloat16)

    gmask = (
        lax.broadcasted_iota(jnp.int32, (ngroups, chunk), 1) // GROUP
        == lax.broadcasted_iota(jnp.int32, (ngroups, chunk), 0)
    )
    zero_row = jnp.zeros((ngroups, chunk), jnp.bfloat16)
    vo_rows = jnp.where(gmask, fld[4:5, :], zero_row)
    uo_rows = jnp.where(gmask, fld[3:4, :], zero_row)
    tlane = lax.broadcasted_iota(jnp.int32, (ngroups, TILE), 1)
    tab_ref[0] = jnp.dot(vo_rows, xv_ref[...], preferred_element_type=jnp.float32).astype(jnp.int32) + tlane % SUPPORT
    tab_ref[1] = jnp.dot(uo_rows, xu_ref[...], preferred_element_type=jnp.float32).astype(jnp.int32) + tlane // GROUP

    rep_ref[...] = weighted.astype(jnp.float32)
    lane = lax.broadcasted_iota(jnp.int32, (GROUP, TILE), 1)
    row = lax.broadcasted_iota(jnp.int32, (GROUP, TILE), 0)
    keep = (lane // SUPPORT) == row
    vrow = lax.broadcasted_iota(jnp.int32, (TILE, TILE), 0)
    urow = lax.broadcasted_iota(jnp.int32, (rows, TILE), 0)
    zero = jnp.zeros((GROUP, TILE), jnp.float32)

    def body(g, carry):
        start = pl.multiple_of(g * GROUP, GROUP)
        halves = [rep_ref[pl.ds(start + h * 8, 8), :] for h in range(GROUP // 8)]
        pre = [pltpu.roll(v, TILE // 2, 1) for v in halves]
        blocks = []
        for i in range(nblocks):
            for h in range(GROUP // 8):
                shift = (h * 8 * SUPPORT - i * SUPPORT) % TILE
                if shift + 7 * SUPPORT < TILE:
                    moved = pltpu.roll(halves[h], shift, 1, stride=SUPPORT, stride_axis=0)
                else:
                    moved = pltpu.roll(pre[h], shift - TILE // 2, 1, stride=SUPPORT, stride_axis=0)
                blocks.append(jnp.where(keep[h * 8:(h + 1) * 8], moved, zero[:8]))
        wbd = jnp.concatenate(blocks, axis=0).astype(jnp.bfloat16)
        vob = tab_ref[0, pl.ds(g, 1), :]
        cst = (vrow == vob).astype(jnp.bfloat16)
        spread = lax.dot_general(
            wbd, cst, (((1,), (1,)), ((), ())), preferred_element_type=jnp.float32
        ).astype(jnp.bfloat16)
        at = pl.multiple_of(g * depth, depth)
        x_ref[0, pl.ds(at, depth), :] = spread[:depth]
        x_ref[1, pl.ds(at, depth), :] = spread[depth:]
        uoa = tab_ref[1, pl.ds(g, 1), :]
        r_ref[:, pl.ds(at, TILE)] = (urow == uoa).astype(jnp.bfloat16)
        return carry

    lax.fori_loop(0, ngroups, body, 0, unroll=True)
    if member_ref is None:
        pick = r_ref[...]
        out_ref[0] += jnp.dot(pick, x_ref[0], preferred_element_type=jnp.float32)
        out_ref[1] += jnp.dot(pick, x_ref[1], preferred_element_type=jnp.float32)
    else:
        part = out_ref.shape[1]
        member = member_ref[0]
        for target, sel in ((out_ref, member), (other_ref, 1 - member)):
            pick = r_ref[pl.ds(pl.multiple_of(sel * part, part), part), :]
            target[0] += jnp.dot(pick, x_ref[0], preferred_element_type=jnp.float32)
            target[1] += jnp.dot(pick, x_ref[1], preferred_element_type=jnp.float32)


def grid_rows(fld, kernels, rows, member=None, full_dests=None):
    dests, nf, per_dest = fld.shape
    chunk = per_dest
    for size in (384, 192, 96, 48, 16):
        if per_dest % size == 0 and size <= per_dest:
            chunk = size
            break
    steps = per_dest // chunk
    ngroups = chunk // GROUP
    width = kernels.shape[1]
    half = width // 2
    nblocks = width // SUPPORT
    eye = (
        lax.broadcasted_iota(jnp.int32, (chunk, chunk), 0)
        == lax.broadcasted_iota(jnp.int32, (chunk, chunk), 1)
    ).astype(jnp.bfloat16)
    table = jnp.concatenate(split3(kernels), axis=1)
    n_in = lax.broadcasted_iota(jnp.int32, (chunk, TILE), 0) % GROUP
    lane_t = lax.broadcasted_iota(jnp.int32, (chunk, TILE), 1)
    expand_v = (n_in == lane_t // SUPPORT).astype(jnp.bfloat16)
    expand_u = (n_in == lane_t % GROUP).astype(jnp.bfloat16)
    whole = lambda d, c: (0, 0)
    scratch = [
        pltpu.VMEM((chunk, width), jnp.float32),
        pltpu.VMEM((2, chunk * SUPPORT, TILE), jnp.bfloat16),
        pltpu.VMEM((rows, chunk * SUPPORT), jnp.bfloat16),
        pltpu.VMEM((2, ngroups, TILE), jnp.int32),
    ]
    params = pltpu.CompilerParams(dimension_semantics=("arbitrary", "arbitrary"))
    operands = (fld, eye, table, expand_v, expand_u)
    if member is None:
        whole = lambda d, c: (0, 0)
        return pl.pallas_call(
            grid_kernel,
            grid=(dests, steps),
            in_specs=[
                pl.BlockSpec((1, nf, chunk), lambda d, c: (d, 0, c)),
                pl.BlockSpec((chunk, chunk), whole),
                pl.BlockSpec(table.shape, whole),
                pl.BlockSpec((chunk, TILE), whole),
                pl.BlockSpec((chunk, TILE), whole),
            ],
            out_specs=[
                pl.BlockSpec((2, rows, TILE), lambda d, c: (0, 0, d)),
                pl.BlockSpec((2, SUPPORT, TILE), lambda d, c: (0, 0, 0)),
            ],
            out_shape=[
                jax.ShapeDtypeStruct((2, rows, dests * TILE), jnp.float32),
                jax.ShapeDtypeStruct((2, SUPPORT, TILE), jnp.float32),
            ],
            scratch_shapes=scratch,
            compiler_params=params,
        )(*operands)[0]
    part = rows // 2
    whole = lambda d, c, m: (0, 0)
    grid_spec = pltpu.PrefetchScalarGridSpec(
        num_scalar_prefetch=1,
        grid=(dests, steps),
        in_specs=[
            pl.BlockSpec((1, nf, chunk), lambda d, c, m: (d, 0, c)),
            pl.BlockSpec((chunk, chunk), whole),
            pl.BlockSpec(table.shape, whole),
            pl.BlockSpec((chunk, TILE), whole),
            pl.BlockSpec((chunk, TILE), whole),
        ],
        out_specs=[
            pl.BlockSpec((2, part, TILE), lambda d, c, m: (0, 0, m[0] * dests + d)),
            pl.BlockSpec((2, part, TILE), lambda d, c, m: (0, 0, d)),
        ],
        scratch_shapes=scratch,
    )
    return pl.pallas_call(
        grid_kernel,
        grid_spec=grid_spec,
        out_shape=[
            jax.ShapeDtypeStruct((2, part, full_dests * TILE), jnp.float32),
            jax.ShapeDtypeStruct((2, part, dests * TILE), jnp.float32),
        ],
        compiler_params=params,
    )(member.reshape(1), *operands)


def shards(visibilities, tile_counts, w_plane, u_offset, v_offset, kernels):
    dests = visibilities.shape[2]
    ntiles = visibilities.shape[3]
    slots = visibilities.shape[4]
    axes = ("uv", "rep")
    ndev = lax.axis_size(axes)
    rows = ntiles * TILE // ndev
    per_tile = ndev // ntiles
    own_dests = dests // per_tile
    me = lax.axis_index(axes)
    member = me % per_tile
    live = (
        lax.broadcasted_iota(jnp.int32, (dests, ntiles, slots), 2) < tile_counts[0][:, :, None]
    ).astype(jnp.float32)
    fields = jnp.concatenate(
        [
            visibilities[0, 0] * live,
            visibilities[1, 0] * live,
            w_plane[0].astype(jnp.float32),
            u_offset[0].astype(jnp.float32),
            v_offset[0].astype(jnp.float32),
        ],
        axis=-1,
    )
    send = fields.reshape(per_tile, own_dests, ntiles, FIELDS * slots).transpose(2, 0, 1, 3)
    send = send.reshape(ndev, own_dests * FIELDS * slots)
    got = lax.all_to_all(send, axes, split_axis=0, concat_axis=0, tiled=True)
    got = got.reshape(ndev, own_dests, FIELDS, slots).transpose(1, 2, 0, 3)
    got = got.reshape(own_dests, FIELDS, ndev * slots)
    got = jnp.pad(got, ((0, 0), (0, 8 - FIELDS), (0, 0)))
    got = jnp.concatenate(split3(got), axis=1)
    width = own_dests * TILE
    if per_tile == 2:
        full, other = grid_rows(got, kernels, TILE, member.astype(jnp.int32), dests)
        other = lax.ppermute(other, axes, [(k, k ^ 1) for k in range(ndev)])
        full = lax.dynamic_update_slice_in_dim(full, other, (1 - member) * width, axis=2)
        return transform(full, dests)
    slab = grid_rows(got, kernels, TILE)
    mine = lax.dynamic_slice_in_dim(slab, member * rows, rows, axis=1)
    full = jnp.zeros((2, rows, dests * TILE), jnp.float32)
    full = lax.dynamic_update_slice_in_dim(full, mine, member * width, axis=2)
    for step in range(1, per_tile):
        target = (member + step) % per_tile
        source = (member + per_tile - step) % per_tile
        pairs = [
            (k, (k // per_tile) * per_tile + (k % per_tile + step) % per_tile)
            for k in range(ndev)
        ]
        piece = lax.dynamic_slice_in_dim(slab, target * rows, rows, axis=1)
        piece = lax.ppermute(piece, axes, pairs)
        full = lax.dynamic_update_slice_in_dim(full, piece, source * width, axis=2)
    return transform(full, dests)


def solution(mesh):
    placed = (
        P(None, ("uv", "rep"), None, None, None),
        P(("uv", "rep"), None, None),
        P(("uv", "rep"), None, None, None),
        P(("uv", "rep"), None, None, None),
        P(("uv", "rep"), None, None, None),
        P(),
    )
    return jax.shard_map(
        shards, mesh=mesh, in_specs=placed, out_specs=P(("uv", "rep"), None, None), check_vma=False
    )
```
